128 devices in a mesh: dp: 16 (over y, x_lo, core), ctx: 8 (over z, x_hi).
Axes of the slice: x: 4 (x_hi: 2, x_lo: 2; x = x_hi * 2 + x_lo), y: 4, z: 4, core: 2. Of those that a mesh axis runs over, the one named last changes fastest.
Arguments:
- query_in: bfloat16 [32768, 2048], P(('dp', 'ctx')), may hold values from -16 to 16
- key_in: bfloat16 [32768, 512], P(('dp', 'ctx')), may hold values from -16 to 16
- value_in: bfloat16 [32768, 512], P(('dp', 'ctx')), may hold values from -6 to 6
- grad_out: bfloat16 [32768, 2048], P(('dp', 'ctx')), may hold values from -6 to 6
- target: int32 [32768], P(('dp', 'ctx')), may hold values from 0 to 32767, as said below
- span_order: int32 [16, 16], P('dp'), may hold values from 0 to 15, each once within a row
- doc_ids: int32 [16, 2048], P('dp', 'ctx'), may hold values from 0 to 7, never falling along the last dimension, each value on 1 to 1024 neighbouring positions
Outputs:
- grad_query: float32 [32768, 2048], P(('dp', 'ctx'))
- grad_key: float32 [32768, 512], P(('dp', 'ctx'))
- grad_value: float32 [32768, 512], P(('dp', 'ctx'))
The draws below stay inside these ranges and needn't reach their ends.
Inputs may be any that keep to these rules, and one draw needn't show every extreme that they name: target is a permutation of the 32768 packed rows; of the 256 rows of one device at most 4 go to any one block of 256 packed rows, and exactly 4 go to some block. `span_order`: each row names every span once. `doc_ids`: each document is one run of 1 to 1024 positions; numbers never fall along a pack.
All inputs are finite; a program needn't handle non-finite values.
Results may differ from the reference program's by a relative error of at most 0.035.
Values may be sent and summed in bfloat16 or wider, within the bound.
No kernel may reach another device: no remote copies, remote signals or barrier semaphores. Data moves between devices by JAX's collectives and lax.ppermute only.
A program may use at most 128 MiB of HBM per device.

```python
import math
import jax
import jax.numpy as jnp
import numpy as np
from jax import lax

TOK_DEV = 256
HQ = 16
HK = 4
DH = 128
DOCS = 8
PACKS = 16
PACK_LEN = 2048
TOKENS = 32768
SPAN = 128
DOC_MOST = 1024
N_CTX = 8


def draw_query_in(key, part):
    noise = jax.random.truncated_normal(jax.random.fold_in(key, 1), -4.0, 4.0, (TOKENS, HQ * DH), jnp.float32)
    return noise.astype(jnp.bfloat16)


def draw_key_in(key, part):
    noise = jax.random.truncated_normal(jax.random.fold_in(key, 3), -4.0, 4.0, (TOKENS, HK * DH), jnp.float32)
    return noise.astype(jnp.bfloat16)


def draw_target(key, part):
    devices = TOKENS // TOK_DEV
    base_count = TOK_DEV // devices
    first_key, second_key, third_key, fourth_key = jax.random.split(jax.random.fold_in(key, 11), 4)
    sigma = jax.random.permutation(first_key, devices)
    shifts = jax.random.permutation(second_key, devices - 1)[:6] + 1
    weights = jnp.array([2, 1, 1, -1, -1, -2], jnp.int32)
    columns = (sigma[:, None] + shifts[None, :]) % devices
    hits = (columns[:, :, None] == jnp.arange(devices)[None, None, :]).astype(jnp.int32)
    counts = base_count + jnp.sum(weights[None, :, None] * hits, axis=1)
    source_incl = jnp.cumsum(counts, axis=1)
    source_excl = source_incl - counts
    dest_excl = jnp.cumsum(counts, axis=0) - counts
    ranks = jnp.arange(TOK_DEV)
    dest_of = jnp.sum((source_incl[:, None, :] <= ranks[None, :, None]).astype(jnp.int32), axis=2)
    within = ranks[None, :] - jnp.take_along_axis(source_excl, dest_of, axis=1)
    dest_rank = jnp.take_along_axis(dest_excl, dest_of, axis=1) + within
    dest_perm = jax.vmap(lambda single: jax.random.permutation(single, TOK_DEV))(jax.random.split(third_key, devices))
    source_perm = jax.vmap(lambda single: jax.random.permutation(single, TOK_DEV))(jax.random.split(fourth_key, devices))
    dest_row = dest_perm[dest_of, dest_rank]
    landing = dest_of * TOK_DEV + dest_row
    arrival = jnp.arange(devices)[:, None] * TOK_DEV + source_perm
    target = jnp.zeros((TOKENS,), jnp.int32).at[arrival.reshape(-1)].set(landing.reshape(-1).astype(jnp.int32))
    return target


def steps_of(stream_key, extent, pieces, smallest, top_value):
    def one(axis_at, shards_of):
        steps = jax.random.uniform(jax.random.fold_in(jax.random.fold_in(stream_key, 6), axis_at), (shards_of,), jnp.float32, smallest / len(pieces), top_value / len(pieces))
        return jnp.repeat(jnp.exp(steps), extent[axis_at] // shards_of).reshape((-1,) + (1,) * (len(extent) - axis_at - 1))

    gain = one(*pieces[0])
    for cut in pieces[1:]:
        gain = gain * one(*cut)
    return gain


def profile(count, total, limit, lean):
    loads = [(1 << 20) // math.isqrt(standing ** lean) + 1 for standing in range(2, count + 1)]
    rest, holding = total - limit - (count - 1), [1] * (count - 1)
    while rest > 0:
        candidates = [i for i in range(count - 1) if holding[i] < limit]
        pool, remaining = sum([loads[i] for i in candidates]), rest
        for i in candidates:
            more = min(limit - holding[i], max(1, remaining * loads[i] // pool), rest)
            holding[i] = holding[i] + more
            rest = rest - more
    return np.array([limit] + holding)


def uneven(stream_key, amount, total, bound, skew):
    if amount == 2:
        one = jax.random.randint(stream_key, (), max(1, total - bound), min(bound, total - 1) + 1)
        return jnp.stack([one, total - one])
    sizes = jnp.asarray(profile(amount, total, bound, skew), jnp.int32)
    twos = (amount - 1) // 2
    source_of, sink = sizes[1:1 + 2 * twos:2], sizes[2:2 + 2 * twos:2]
    room = jnp.minimum(source_of - 1, bound - sink)
    shifted = jax.random.randint(jax.random.fold_in(stream_key, 1), (twos,), 0, 1 << 20) % (room + 1)
    sizes = sizes.at[1:1 + 2 * twos:2].set(source_of - shifted).at[2:2 + 2 * twos:2].set(sink + shifted)
    return sizes[jax.random.permutation(jax.random.fold_in(stream_key, 2), amount)]


def gaussian(own_key, extent, spread, bound, shards=(), kind=jnp.bfloat16):
    values = spread * jax.random.normal(own_key, extent, jnp.float32)
    if shards:
        values = values * steps_of(own_key, extent, shards, -0.22, 0.18)
    return jnp.clip(values, -bound, bound).astype(kind)


def setup_inputs(seed: int = 0) -> dict:
    seeds = jax.random.split(jax.random.key(seed), 8)
    return {
        "query_in": draw_query_in(jax.random.fold_in(seeds[7], 71), 0),
        "key_in": draw_key_in(jax.random.fold_in(seeds[7], 71), 0),
        "value_in": gaussian(seeds[2], (TOKENS, HK * DH), 1.0, 6.0, ((0, 128),)),
        "grad_out": gaussian(seeds[3], (TOKENS, HQ * DH), 1.0, 6.0, ((0, 128),)),
        "target": draw_target(jax.random.fold_in(seeds[7], 71), 0),
        "span_order": jax.vmap(lambda own: jax.random.permutation(own, 2 * N_CTX))(jax.random.split(seeds[5], PACKS)).reshape((PACKS, 2 * N_CTX)).astype(jnp.int32),
        "doc_ids": jax.vmap(lambda own: jnp.searchsorted(jnp.cumsum(uneven(own, DOCS, PACK_LEN, DOC_MOST, 2)), jnp.arange(PACK_LEN), side="right"))(jax.random.split(seeds[6], PACKS)).reshape((PACKS, PACK_LEN)).astype(jnp.int32),
    }


def rounded(values):
    return lax.optimization_barrier(values.astype(jnp.bfloat16)).astype(jnp.float32)


def head_group(inputs, allowed):
    queries, keys, values, grads = inputs
    highest = lax.Precision.HIGHEST
    score_scale = DH ** -0.5
    scores = jnp.einsum("qgd,kd->gqk", queries, keys, precision=highest) * score_scale
    scores = jnp.where(allowed[None], scores, -jnp.inf)
    row_max = jnp.max(scores, axis=-1, keepdims=True)
    log_norm = row_max + jnp.log(jnp.sum(jnp.exp(scores - row_max), axis=-1, keepdims=True))
    probs = jnp.exp(scores - log_norm)
    probs_low = rounded(probs)
    attended = rounded(jnp.einsum("gqk,kd->qgd", probs_low, values, precision=highest))
    delta = jnp.sum(grads * attended, axis=-1).T[:, :, None]
    dprobs = jnp.einsum("qgd,kd->gqk", grads, values, precision=highest)
    dscore_low = rounded(probs * (dprobs - delta))
    dquery = jnp.einsum("gqk,kd->qgd", dscore_low, keys, precision=highest) * score_scale
    dkey = jnp.einsum("gqk,qgd->kd", dscore_low, queries, precision=highest) * score_scale
    dvalue = jnp.einsum("gqk,qgd->kd", probs_low, grads, precision=highest)
    return dquery, dkey, dvalue


def one_pack(inputs):
    queries, keys, values, grads, positions, documents = inputs
    groups = HQ // HK
    allowed = (positions[None, :] <= positions[:, None]) & (documents[None, :] == documents[:, None])
    query_heads = queries.astype(jnp.float32).reshape(PACK_LEN, HK, groups, DH).transpose(1, 0, 2, 3)
    grad_heads = grads.astype(jnp.float32).reshape(PACK_LEN, HK, groups, DH).transpose(1, 0, 2, 3)
    key_heads = keys.astype(jnp.float32).reshape(PACK_LEN, HK, DH).transpose(1, 0, 2)
    value_heads = values.astype(jnp.float32).reshape(PACK_LEN, HK, DH).transpose(1, 0, 2)

    def per_head(stacked):
        return head_group(stacked, allowed)

    dquery, dkey, dvalue = lax.map(per_head, (query_heads, key_heads, value_heads, grad_heads))
    dquery = dquery.transpose(1, 0, 2, 3).reshape(PACK_LEN, HQ * DH)
    dkey = dkey.transpose(1, 0, 2).reshape(PACK_LEN, HK * DH)
    dvalue = dvalue.transpose(1, 0, 2).reshape(PACK_LEN, HK * DH)
    return dquery, dkey, dvalue


def reference(query_in, key_in, value_in, grad_out, target, span_order, doc_ids):
    def to_packed(values):
        return jnp.zeros_like(values).at[target].set(values).reshape((PACKS, PACK_LEN) + values.shape[1:])

    offsets = jnp.arange(SPAN, dtype=jnp.int32)
    positions = (span_order[:, :, None] * SPAN + offsets[None, None, :]).reshape(PACKS, PACK_LEN).astype(jnp.int32)
    documents = jnp.take_along_axis(doc_ids, positions, axis=1)
    dquery, dkey, dvalue = lax.map(one_pack, (to_packed(query_in), to_packed(key_in), to_packed(value_in), to_packed(grad_out), positions, documents))
    grad_query = dquery.reshape(TOKENS, HQ * DH)[target]
    grad_key = dkey.reshape(TOKENS, HK * DH)[target]
    grad_value = dvalue.reshape(TOKENS, HK * DH)[target]
    return grad_query, grad_key, grad_value
```

```python
import jax
import jax.numpy as jnp
from jax import lax
from jax.sharding import PartitionSpec as P

HQ = 16
HK = 4
DH = 128


block_keys = 512


def visible(query_pos, query_doc, key_pos, key_doc):
    return (key_pos[None, :] <= query_pos[:, None]) & (key_doc[None, :] == query_doc[:, None])


def masked_scores(query_blk, key_blk, allowed):
    raw_scores = jnp.einsum(
        "qhgd,khd->hgqk", query_blk, key_blk, preferred_element_type=jnp.float32
    ) * DH ** (-0.5)
    return jnp.where(allowed[None, None], raw_scores, -jnp.inf)


def grad_terms(query_blk, grad_blk, lse_blk, delta_blk, key_blk, value_blk, allowed):
    scores = masked_scores(query_blk, key_blk, allowed)
    probs = jnp.exp(scores - lse_blk[..., None])
    probs_low = probs.astype(jnp.bfloat16)
    dprobs = jnp.einsum("qhgd,khd->hgqk", grad_blk, value_blk, preferred_element_type=jnp.float32)
    dscore_low = (probs * (dprobs - delta_blk[..., None])).astype(jnp.bfloat16)
    return (probs_low, dscore_low)


def local(query_in, key_in, value_in, grad_out, target, span_order, doc_ids):
    local_rows = query_in.shape[0]
    devices = lax.axis_size(("dp", "ctx"))
    ctx_size = lax.axis_size("ctx")
    capacity = local_rows // devices + 2
    groups = HQ // HK
    score_scale = DH ** (-0.5)
    q_cols = query_in.shape[1]
    k_cols = key_in.shape[1]
    owners = target // local_rows
    onehot = (owners[:, None] == jnp.arange(devices, dtype=jnp.int32)[None, :]).astype(jnp.int32)
    earlier = jnp.cumsum(onehot, axis=0) - onehot
    slot_ids = owners * capacity + jnp.sum(earlier * onehot, axis=1)

    place_col = jnp.zeros((local_rows, 128), jnp.bfloat16).at[:, 0].set(
        (target % local_rows + 1).astype(jnp.bfloat16)
    )
    payload = jnp.concatenate([query_in, key_in, value_in, grad_out, place_col], axis=1)
    width = payload.shape[1]
    holder = jnp.zeros((devices * capacity, width), jnp.bfloat16).at[slot_ids].set(payload)
    got = lax.all_to_all(
        holder.reshape(devices, capacity, width), ("dp", "ctx"), split_axis=0, concat_axis=0, tiled=True
    ).reshape(devices * capacity, width)
    arrived = got[:, 2 * q_cols + 2 * k_cols].astype(jnp.int32) - 1
    landing = jnp.where(arrived >= 0, arrived, local_rows)
    rows = jnp.zeros((local_rows, width), jnp.bfloat16).at[landing].set(got, mode="drop")
    query = rows[:, :q_cols]
    kv_rows = rows[:, q_cols : q_cols + 2 * k_cols]
    grad_rows = rows[:, q_cols + 2 * k_cols : 2 * q_cols + 2 * k_cols]

    span_rows = local_rows // 2
    span_seq = span_order[0]
    pack_len = local_rows * ctx_size
    positions = (
        span_seq[:, None] * span_rows + jnp.arange(span_rows, dtype=jnp.int32)[None, :]
    ).reshape(-1)
    ctx_index = lax.axis_index("ctx")
    own_pos = lax.dynamic_slice_in_dim(positions, ctx_index * local_rows, local_rows)
    doc_col = jnp.zeros((local_rows, 128), jnp.bfloat16).at[:, 0].set(doc_ids[0].astype(jnp.bfloat16))
    gathered = lax.all_gather(
        jnp.concatenate([kv_rows, doc_col], axis=1), "ctx", axis=0, tiled=True
    )
    seq_docs = gathered[:, 2 * k_cols].astype(jnp.int32)
    doc_all = seq_docs.reshape(2 * ctx_size, span_rows)[span_seq].reshape(-1)
    own_docs = lax.dynamic_slice_in_dim(doc_all, ctx_index * local_rows, local_rows)
    query_heads = query.reshape(local_rows, HK, groups, DH)
    grad_heads = grad_rows.reshape(local_rows, HK, groups, DH)
    key_heads = gathered[:, :k_cols].reshape(pack_len, HK, DH)
    value_heads = gathered[:, k_cols : 2 * k_cols].reshape(pack_len, HK, DH)
    num_blocks = pack_len // block_keys

    def key_block(block_index):
        first_key = block_index * block_keys
        return (
            lax.dynamic_slice_in_dim(key_heads, first_key, block_keys),
            lax.dynamic_slice_in_dim(value_heads, first_key, block_keys),
            lax.dynamic_slice_in_dim(positions, first_key, block_keys),
            lax.dynamic_slice_in_dim(doc_all, first_key, block_keys),
        )

    def stats_step(block_index, carry):
        key_blk, value_blk, key_pos, key_doc = key_block(block_index)
        allowed = visible(own_pos, own_docs, key_pos, key_doc)
        running_max, running_sum = carry
        scores = masked_scores(query_heads, key_blk, allowed)
        new_max = jnp.maximum(running_max, jnp.max(scores, axis=-1))
        rescale = jnp.exp(running_max - new_max)
        running_sum = running_sum * rescale + jnp.sum(jnp.exp(scores - new_max[..., None]), axis=-1)
        return (new_max, running_sum)

    start_stats = (
        jnp.full((HK, groups, local_rows), -1e30, jnp.float32),
        jnp.zeros((HK, groups, local_rows), jnp.float32),
    )
    running_max, running_sum = lax.fori_loop(0, num_blocks, stats_step, start_stats)
    log_norm = running_max + jnp.log(running_sum)

    def output_step(block_index, carry):
        key_blk, value_blk, key_pos, key_doc = key_block(block_index)
        allowed = visible(own_pos, own_docs, key_pos, key_doc)
        scores = masked_scores(query_heads, key_blk, allowed)
        probs_low = jnp.exp(scores - log_norm[..., None]).astype(jnp.bfloat16)
        return carry + jnp.einsum(
            "hgqk,khd->qhgd", probs_low, value_blk, preferred_element_type=jnp.float32
        )

    summed = lax.fori_loop(
        0, num_blocks, output_step, jnp.zeros((local_rows, HK, groups, DH), jnp.float32)
    )
    attended_low = summed.astype(jnp.bfloat16)
    delta = jnp.sum(
        grad_heads.astype(jnp.float32) * attended_low.astype(jnp.float32), axis=-1
    ).transpose(1, 2, 0)

    def back_step(block_index, carry):
        key_blk, value_blk, key_pos, key_doc = key_block(block_index)
        allowed = visible(own_pos, own_docs, key_pos, key_doc)
        dquery, dkey_all, dvalue_all = carry
        probs_low, dscore_low = grad_terms(
            query_heads, grad_heads, log_norm, delta, key_blk, value_blk, allowed
        )
        dquery = dquery + jnp.einsum(
            "hgqk,khd->qhgd", dscore_low, key_blk, preferred_element_type=jnp.float32
        )
        dkey = (
            jnp.einsum(
                "hgqk,qhgd->khd", dscore_low, query_heads, preferred_element_type=jnp.float32
            )
            * score_scale
        )
        dvalue = jnp.einsum(
            "hgqk,qhgd->khd", probs_low, grad_heads, preferred_element_type=jnp.float32
        )
        first_key = block_index * block_keys
        dkey_all = lax.dynamic_update_slice_in_dim(
            dkey_all, dkey.reshape(block_keys, HK * DH), first_key, 0
        )
        dvalue_all = lax.dynamic_update_slice_in_dim(
            dvalue_all, dvalue.reshape(block_keys, HK * DH), first_key, 0
        )
        return (dquery, dkey_all, dvalue_all)

    start_back = (
        jnp.zeros((local_rows, HK, groups, DH), jnp.float32),
        jnp.zeros((pack_len, HK * DH), jnp.float32),
        jnp.zeros((pack_len, HK * DH), jnp.float32),
    )
    dquery, dkey_all, dvalue_all = lax.fori_loop(0, num_blocks, back_step, start_back)
    partial = jnp.concatenate([dkey_all, dvalue_all], axis=1).astype(jnp.bfloat16)
    summed_kv = jnp.sum(
        lax.all_to_all(
            partial.reshape(ctx_size, local_rows, 2 * k_cols), "ctx", split_axis=0, concat_axis=0, tiled=True
        ).astype(jnp.float32),
        axis=0,
    )
    dquery_full = (dquery * score_scale).reshape(local_rows, HQ * DH)
    source_rows = jnp.where(arrived >= 0, arrived, 0)
    result = jnp.concatenate([dquery_full.astype(jnp.bfloat16), summed_kv.astype(jnp.bfloat16)], axis=1)
    back = lax.all_to_all(
        result[source_rows].reshape(devices, capacity, q_cols + 2 * k_cols),
        ("dp", "ctx"),
        split_axis=0,
        concat_axis=0,
        tiled=True,
    ).reshape(devices * capacity, q_cols + 2 * k_cols)[slot_ids].astype(jnp.float32)
    return (back[:, :q_cols], back[:, q_cols : q_cols + k_cols], back[:, q_cols + k_cols :])


def solution(mesh):
    placed = (
        P(("dp", "ctx"), None),
        P(("dp", "ctx"), None),
        P(("dp", "ctx"), None),
        P(("dp", "ctx"), None),
        P(("dp", "ctx")),
        P("dp", None),
        P("dp", "ctx"),
    )
    return jax.shard_map(
        local,
        mesh=mesh,
        in_specs=placed,
        out_specs=(P(("dp", "ctx"), None), P(("dp", "ctx"), None), P(("dp", "ctx"), None)),
        check_vma=False,
    )
```

```python
import jax
import jax.numpy as jnp
from jax import lax
from jax.sharding import PartitionSpec as P

HQ = 16
HK = 4
DH = 128


block_keys = 128


def visible(query_pos, query_doc, key_pos, key_doc):
    return (key_pos[None, :] <= query_pos[:, None]) & (key_doc[None, :] == query_doc[:, None])


def masked_scores(query_blk, key_blk, allowed):
    raw_scores = jnp.einsum(
        "qhgd,khd->hgqk", query_blk, key_blk, preferred_element_type=jnp.float32
    ) * DH ** (-0.5)
    return jnp.where(allowed[None, None], raw_scores, -jnp.inf)


def grad_terms(query_blk, grad_blk, lse_blk, delta_blk, key_blk, value_blk, allowed):
    scores = masked_scores(query_blk, key_blk, allowed)
    probs = jnp.exp(scores - lse_blk[..., None])
    probs_low = probs.astype(jnp.bfloat16)
    dprobs = jnp.einsum("qhgd,khd->hgqk", grad_blk, value_blk, preferred_element_type=jnp.float32)
    dscore_low = (probs * (dprobs - delta_blk[..., None])).astype(jnp.bfloat16)
    return (probs_low, dscore_low)


def local(query_in, key_in, value_in, grad_out, target, span_order, doc_ids):
    local_rows = query_in.shape[0]
    devices = lax.axis_size(("dp", "ctx"))
    ctx_size = lax.axis_size("ctx")
    capacity = local_rows // devices + 2
    groups = HQ // HK
    score_scale = DH ** (-0.5)
    q_cols = query_in.shape[1]
    k_cols = key_in.shape[1]
    owners = target // local_rows
    onehot = (owners[:, None] == jnp.arange(devices, dtype=jnp.int32)[None, :]).astype(jnp.int32)
    earlier = jnp.cumsum(onehot, axis=0) - onehot
    slot_ids = owners * capacity + jnp.sum(earlier * onehot, axis=1)

    place_col = jnp.zeros((local_rows, 128), jnp.bfloat16).at[:, 0].set(
        (target % local_rows + 1).astype(jnp.bfloat16)
    )

    def exchange(payload):
        width = payload.shape[1]
        holder = jnp.zeros((devices * capacity, width), payload.dtype).at[slot_ids].set(payload)
        return lax.all_to_all(
            holder.reshape(devices, capacity, width), ("dp", "ctx"), split_axis=0, concat_axis=0, tiled=True
        ).reshape(devices * capacity, width)

    got_kv = exchange(jnp.concatenate([key_in, value_in, place_col], axis=1))
    got_qg = exchange(jnp.concatenate([query_in, grad_out], axis=1))
    arrived = got_kv[:, 2 * k_cols].astype(jnp.int32) - 1
    landing = jnp.where(arrived >= 0, arrived, local_rows)

    def unpack(values):
        return jnp.zeros((local_rows, values.shape[1]), values.dtype).at[landing].set(values, mode="drop")

    kv_rows = unpack(got_kv[:, : 2 * k_cols])
    qg_rows = unpack(got_qg)
    query = qg_rows[:, :q_cols]
    grad_rows = qg_rows[:, q_cols:]

    span_rows = local_rows // 2
    span_seq = span_order[0]
    pack_len = local_rows * ctx_size
    positions = (
        span_seq[:, None] * span_rows + jnp.arange(span_rows, dtype=jnp.int32)[None, :]
    ).reshape(-1)
    ctx_index = lax.axis_index("ctx")
    own_pos = lax.dynamic_slice_in_dim(positions, ctx_index * local_rows, local_rows)
    doc_col = jnp.zeros((local_rows, 128), jnp.bfloat16).at[:, 0].set(doc_ids[0].astype(jnp.bfloat16))
    gathered = lax.all_gather(
        jnp.concatenate([kv_rows, doc_col], axis=1), "ctx", axis=0, tiled=True
    )
    seq_docs = gathered[:, 2 * k_cols].astype(jnp.int32)
    doc_all = seq_docs.reshape(2 * ctx_size, span_rows)[span_seq].reshape(-1)
    own_docs = lax.dynamic_slice_in_dim(doc_all, ctx_index * local_rows, local_rows)
    query_heads = query.reshape(local_rows, HK, groups, DH)
    grad_heads = grad_rows.reshape(local_rows, HK, groups, DH)
    key_heads = gathered[:, :k_cols].reshape(pack_len, HK, DH)
    value_heads = gathered[:, k_cols : 2 * k_cols].reshape(pack_len, HK, DH)
    num_blocks = pack_len // block_keys
    allowed_all = visible(own_pos, own_docs, positions, doc_all)
    active = jnp.any(allowed_all.reshape(local_rows, num_blocks, block_keys), axis=(0, 2))
    n_active = jnp.sum(active.astype(jnp.int32))
    rank = jnp.cumsum(active.astype(jnp.int32)) - 1
    block_list = (
        jnp.zeros((num_blocks,), jnp.int32)
        .at[jnp.where(active, rank, num_blocks)]
        .set(jnp.arange(num_blocks, dtype=jnp.int32), mode="drop")
    )

    def key_block(step):
        first_key = block_list[step] * block_keys
        return (
            lax.dynamic_slice_in_dim(key_heads, first_key, block_keys),
            lax.dynamic_slice_in_dim(value_heads, first_key, block_keys),
            lax.dynamic_slice_in_dim(allowed_all, first_key, block_keys, axis=1),
        )

    def stats_step(block_index, carry):
        key_blk, value_blk, allowed = key_block(block_index)
        running_max, running_sum = carry
        scores = masked_scores(query_heads, key_blk, allowed)
        new_max = jnp.maximum(running_max, jnp.max(scores, axis=-1))
        rescale = jnp.exp(running_max - new_max)
        running_sum = running_sum * rescale + jnp.sum(jnp.exp(scores - new_max[..., None]), axis=-1)
        return (new_max, running_sum)

    start_stats = (
        jnp.full((HK, groups, local_rows), -1e30, jnp.float32),
        jnp.zeros((HK, groups, local_rows), jnp.float32),
    )
    running_max, running_sum = lax.fori_loop(0, n_active, stats_step, start_stats)
    log_norm = running_max + jnp.log(running_sum)

    def output_step(block_index, carry):
        key_blk, value_blk, allowed = key_block(block_index)
        scores = masked_scores(query_heads, key_blk, allowed)
        probs_low = jnp.exp(scores - log_norm[..., None]).astype(jnp.bfloat16)
        return carry + jnp.einsum(
            "hgqk,khd->qhgd", probs_low, value_blk, preferred_element_type=jnp.float32
        )

    summed = lax.fori_loop(
        0, n_active, output_step, jnp.zeros((local_rows, HK, groups, DH), jnp.float32)
    )
    attended_low = summed.astype(jnp.bfloat16)
    delta = jnp.sum(
        grad_heads.astype(jnp.float32) * attended_low.astype(jnp.float32), axis=-1
    ).transpose(1, 2, 0)

    def back_step(block_index, carry):
        key_blk, value_blk, allowed = key_block(block_index)
        dquery, dkey_all, dvalue_all = carry
        probs_low, dscore_low = grad_terms(
            query_heads, grad_heads, log_norm, delta, key_blk, value_blk, allowed
        )
        dquery = dquery + jnp.einsum(
            "hgqk,khd->qhgd", dscore_low, key_blk, preferred_element_type=jnp.float32
        )
        dkey = (
            jnp.einsum(
                "hgqk,qhgd->khd", dscore_low, query_heads, preferred_element_type=jnp.float32
            )
            * score_scale
        )
        dvalue = jnp.einsum(
            "hgqk,qhgd->khd", probs_low, grad_heads, preferred_element_type=jnp.float32
        )
        first_key = block_list[block_index] * block_keys
        dkey_all = lax.dynamic_update_slice_in_dim(
            dkey_all, dkey.reshape(block_keys, HK * DH), first_key, 0
        )
        dvalue_all = lax.dynamic_update_slice_in_dim(
            dvalue_all, dvalue.reshape(block_keys, HK * DH), first_key, 0
        )
        return (dquery, dkey_all, dvalue_all)

    start_back = (
        jnp.zeros((local_rows, HK, groups, DH), jnp.float32),
        jnp.zeros((pack_len, HK * DH), jnp.float32),
        jnp.zeros((pack_len, HK * DH), jnp.float32),
    )
    dquery, dkey_all, dvalue_all = lax.fori_loop(0, n_active, back_step, start_back)
    partial = jnp.concatenate([dkey_all, dvalue_all], axis=1).astype(jnp.bfloat16)
    summed_kv = jnp.sum(
        lax.all_to_all(
            partial.reshape(ctx_size, local_rows, 2 * k_cols), "ctx", split_axis=0, concat_axis=0, tiled=True
        ).astype(jnp.float32),
        axis=0,
    )
    dquery_full = (dquery * score_scale).reshape(local_rows, HQ * DH)
    source_rows = jnp.where(arrived >= 0, arrived, 0)
    result = jnp.concatenate([dquery_full.astype(jnp.bfloat16), summed_kv.astype(jnp.bfloat16)], axis=1)
    back = lax.all_to_all(
        result[source_rows].reshape(devices, capacity, q_cols + 2 * k_cols),
        ("dp", "ctx"),
        split_axis=0,
        concat_axis=0,
        tiled=True,
    ).reshape(devices * capacity, q_cols + 2 * k_cols)[slot_ids].astype(jnp.float32)
    return (back[:, :q_cols], back[:, q_cols : q_cols + k_cols], back[:, q_cols + k_cols :])


def solution(mesh):
    placed = (
        P(("dp", "ctx"), None),
        P(("dp", "ctx"), None),
        P(("dp", "ctx"), None),
        P(("dp", "ctx"), None),
        P(("dp", "ctx")),
        P("dp", None),
        P("dp", "ctx"),
    )
    return jax.shard_map(
        local,
        mesh=mesh,
        in_specs=placed,
        out_specs=(P(("dp", "ctx"), None), P(("dp", "ctx"), None), P(("dp", "ctx"), None)),
        check_vma=False,
    )
```

```python
import jax
import jax.numpy as jnp
from jax import lax
from jax.sharding import PartitionSpec as P
from jax.experimental import pallas as pl
from jax.experimental.pallas import tpu as pltpu

HQ = 16
HK = 4
DH = 128


CHUNK = 256


def attention_kernel(
    list_ref, count_ref, q_ref, g_ref, k_ref, v_ref, qpos_ref, qdoc_ref, kpos_ref, kdoc_ref, dq_ref, dk_ref, dv_ref
):
    scale = DH ** (-0.5)
    rows = q_ref.shape[0]
    count = count_ref[0]
    dk_ref[...] = jnp.zeros(dk_ref.shape, jnp.float32)
    dv_ref[...] = jnp.zeros(dv_ref.shape, jnp.float32)
    qpos = qpos_ref[...]
    qdoc = qdoc_ref[...]

    def chunk(i):
        start = pl.multiple_of(list_ref[i] * CHUNK, CHUNK)
        kp = kpos_ref[:, pl.ds(start, CHUNK)]
        kd = kdoc_ref[:, pl.ds(start, CHUNK)]
        allowed = (kp <= qpos) & (kd == qdoc)
        return start, k_ref[pl.ds(start, CHUNK), :], v_ref[pl.ds(start, CHUNK), :], allowed

    def scores(q, kb, allowed):
        s = lax.dot_general(q, kb, (((1,), (1,)), ((), ())), preferred_element_type=jnp.float32) * scale
        return jnp.where(allowed, s, -jnp.inf)

    for g in range(q_ref.shape[1] // DH):
        cols = slice(g * DH, (g + 1) * DH)
        q = q_ref[:, cols]
        gr = g_ref[:, cols]

        def stats(i, carry):
            m, l = carry
            _, kb, _, allowed = chunk(i)
            s = scores(q, kb, allowed)
            m_new = jnp.maximum(m, jnp.max(s, axis=1, keepdims=True))
            l = l * jnp.exp(m - m_new) + jnp.sum(jnp.exp(s - m_new), axis=1, keepdims=True)
            return m_new, l

        m, l = lax.fori_loop(
            0, count, stats, (jnp.full((rows, 1), -1e30, jnp.float32), jnp.zeros((rows, 1), jnp.float32))
        )
        lse = m + jnp.log(l)

        def forward(i, o):
            _, kb, vb, allowed = chunk(i)
            p = jnp.exp(scores(q, kb, allowed) - lse).astype(jnp.bfloat16)
            return o + jnp.dot(p, vb, preferred_element_type=jnp.float32)

        o = lax.fori_loop(0, count, forward, jnp.zeros((rows, DH), jnp.float32))
        delta = jnp.sum(
            gr.astype(jnp.float32) * o.astype(jnp.bfloat16).astype(jnp.float32), axis=1, keepdims=True
        )

        def backward(i, dq):
            start, kb, vb, allowed = chunk(i)
            p = jnp.exp(scores(q, kb, allowed) - lse)
            dp = lax.dot_general(gr, vb, (((1,), (1,)), ((), ())), preferred_element_type=jnp.float32)
            ds = (p * (dp - delta)).astype(jnp.bfloat16)
            dk_ref[pl.ds(start, CHUNK), :] += lax.dot_general(
                ds, q, (((0,), (0,)), ((), ())), preferred_element_type=jnp.float32
            )
            dv_ref[pl.ds(start, CHUNK), :] += lax.dot_general(
                p.astype(jnp.bfloat16), gr, (((0,), (0,)), ((), ())), preferred_element_type=jnp.float32
            )
            return dq + jnp.dot(ds, kb, preferred_element_type=jnp.float32)

        dq = lax.fori_loop(0, count, backward, jnp.zeros((rows, DH), jnp.float32))
        dq_ref[:, cols] = dq * scale
    dk_ref[...] = dk_ref[...] * scale


def attention(chunk_list, chunk_count, query, grad, keys, values, qpos, qdoc, kpos, kdoc, interpret=False):
    rows, width = query.shape
    keys_len, kv_width = keys.shape
    groups = width // kv_width
    heads = kv_width // DH
    q_spec = pl.BlockSpec((rows, groups * DH), lambda c, *_: (0, c))
    k_spec = pl.BlockSpec((keys_len, DH), lambda c, *_: (0, c))
    col_spec = pl.BlockSpec((rows, 1), lambda c, *_: (0, 0))
    row_spec = pl.BlockSpec((1, keys_len), lambda c, *_: (0, 0))
    return pl.pallas_call(
        attention_kernel,
        grid_spec=pltpu.PrefetchScalarGridSpec(
            num_scalar_prefetch=2,
            grid=(heads,),
            in_specs=[q_spec, q_spec, k_spec, k_spec, col_spec, col_spec, row_spec, row_spec],
            out_specs=[q_spec, k_spec, k_spec],
        ),
        out_shape=[
            jax.ShapeDtypeStruct((rows, width), jnp.float32),
            jax.ShapeDtypeStruct((keys_len, kv_width), jnp.float32),
            jax.ShapeDtypeStruct((keys_len, kv_width), jnp.float32),
        ],
        compiler_params=pltpu.CompilerParams(dimension_semantics=("arbitrary",)),
        interpret=interpret,
    )(chunk_list, chunk_count, query, grad, keys, values, qpos, qdoc, kpos, kdoc)


def visible(query_pos, query_doc, key_pos, key_doc):
    return (key_pos[None, :] <= query_pos[:, None]) & (key_doc[None, :] == query_doc[:, None])


def local(query_in, key_in, value_in, grad_out, target, span_order, doc_ids):
    local_rows = query_in.shape[0]
    devices = lax.axis_size(("dp", "ctx"))
    ctx_size = lax.axis_size("ctx")
    capacity = local_rows // devices + 2
    groups = HQ // HK
    score_scale = DH ** (-0.5)
    q_cols = query_in.shape[1]
    k_cols = key_in.shape[1]
    owners = target // local_rows
    onehot = (owners[:, None] == jnp.arange(devices, dtype=jnp.int32)[None, :]).astype(jnp.int32)
    earlier = jnp.cumsum(onehot, axis=0) - onehot
    slot_ids = owners * capacity + jnp.sum(earlier * onehot, axis=1)

    place_col = jnp.zeros((local_rows, 128), jnp.bfloat16).at[:, 0].set(
        (target % local_rows + 1).astype(jnp.bfloat16)
    )

    def exchange(payload):
        width = payload.shape[1]
        holder = jnp.zeros((devices * capacity, width), payload.dtype).at[slot_ids].set(payload)
        return lax.all_to_all(
            holder.reshape(devices, capacity, width), ("dp", "ctx"), split_axis=0, concat_axis=0, tiled=True
        ).reshape(devices * capacity, width)

    got_kv = exchange(jnp.concatenate([key_in, value_in, place_col], axis=1))
    got_qg = exchange(jnp.concatenate([query_in, grad_out], axis=1))
    arrived = got_kv[:, 2 * k_cols].astype(jnp.int32) - 1
    landing = jnp.where(arrived >= 0, arrived, local_rows)

    def unpack(values):
        return jnp.zeros((local_rows, values.shape[1]), values.dtype).at[landing].set(values, mode="drop")

    kv_rows = unpack(got_kv[:, : 2 * k_cols])
    qg_rows = unpack(got_qg)
    query = qg_rows[:, :q_cols]
    grad_rows = qg_rows[:, q_cols:]

    span_rows = local_rows // 2
    span_seq = span_order[0]
    pack_len = local_rows * ctx_size
    positions = (
        span_seq[:, None] * span_rows + jnp.arange(span_rows, dtype=jnp.int32)[None, :]
    ).reshape(-1)
    ctx_index = lax.axis_index("ctx")
    own_pos = lax.dynamic_slice_in_dim(positions, ctx_index * local_rows, local_rows)
    doc_col = jnp.zeros((local_rows, 128), jnp.bfloat16).at[:, 0].set(doc_ids[0].astype(jnp.bfloat16))
    gathered = lax.all_gather(
        jnp.concatenate([kv_rows, doc_col], axis=1), "ctx", axis=0, tiled=True
    )
    seq_docs = gathered[:, 2 * k_cols].astype(jnp.int32)
    doc_all = seq_docs.reshape(2 * ctx_size, span_rows)[span_seq].reshape(-1)
    own_docs = lax.dynamic_slice_in_dim(doc_all, ctx_index * local_rows, local_rows)
    keys_all = gathered[:, :k_cols]
    values_all = gathered[:, k_cols : 2 * k_cols]
    num_chunks = pack_len // CHUNK
    allowed_all = visible(own_pos, own_docs, positions, doc_all)
    active = jnp.any(allowed_all.reshape(local_rows, num_chunks, CHUNK), axis=(0, 2))
    chunk_count = jnp.sum(active.astype(jnp.int32)).reshape(1)
    rank = jnp.cumsum(active.astype(jnp.int32)) - 1
    chunk_list = (
        jnp.zeros((num_chunks,), jnp.int32)
        .at[jnp.where(active, rank, num_chunks)]
        .set(jnp.arange(num_chunks, dtype=jnp.int32), mode="drop")
    )
    dquery_full, dkey_all, dvalue_all = attention(
        chunk_list,
        chunk_count,
        query,
        grad_rows,
        keys_all,
        values_all,
        own_pos.reshape(local_rows, 1),
        own_docs.reshape(local_rows, 1),
        positions.reshape(1, pack_len),
        doc_all.reshape(1, pack_len),
    )
    partial = jnp.concatenate([dkey_all, dvalue_all], axis=1).astype(jnp.bfloat16)
    summed_kv = jnp.sum(
        lax.all_to_all(
            partial.reshape(ctx_size, local_rows, 2 * k_cols), "ctx", split_axis=0, concat_axis=0, tiled=True
        ).astype(jnp.float32),
        axis=0,
    )
    source_rows = jnp.where(arrived >= 0, arrived, 0)
    result = jnp.concatenate([dquery_full.astype(jnp.bfloat16), summed_kv.astype(jnp.bfloat16)], axis=1)
    back = lax.all_to_all(
        result[source_rows].reshape(devices, capacity, q_cols + 2 * k_cols),
        ("dp", "ctx"),
        split_axis=0,
        concat_axis=0,
        tiled=True,
    ).reshape(devices * capacity, q_cols + 2 * k_cols)[slot_ids].astype(jnp.float32)
    return (back[:, :q_cols], back[:, q_cols : q_cols + k_cols], back[:, q_cols + k_cols :])


def solution(mesh):
    placed = (
        P(("dp", "ctx"), None),
        P(("dp", "ctx"), None),
        P(("dp", "ctx"), None),
        P(("dp", "ctx"), None),
        P(("dp", "ctx")),
        P("dp", None),
        P("dp", "ctx"),
    )
    return jax.shard_map(
        local,
        mesh=mesh,
        in_specs=placed,
        out_specs=(P(("dp", "ctx"), None), P(("dp", "ctx"), None), P(("dp", "ctx"), None)),
        check_vma=False,
    )
```

```python
import jax
import jax.numpy as jnp
from jax import lax
from jax.sharding import PartitionSpec as P
from jax.experimental import pallas as pl
from jax.experimental.pallas import tpu as pltpu

HQ = 16
HK = 4
DH = 128


SPAN_ROWS = 128


def attention_kernel(
    list_ref, count_ref, q_ref, g_ref, k_ref, v_ref, qpos_ref, qdoc_ref, kpos_ref, kdoc_ref,
    dq_ref, dk_ref, dv_ref, tiles_ref,
):
    scale = DH ** (-0.5)
    rows = q_ref.shape[0]
    span = pl.program_id(1)
    spans = list_ref.shape[0] // pl.num_programs(1)
    count = count_ref[span]

    @pl.when(span == 0)
    def _():
        dk_ref[...] = jnp.zeros(dk_ref.shape, jnp.float32)
        dv_ref[...] = jnp.zeros(dv_ref.shape, jnp.float32)

    qpos = qpos_ref[...]
    qdoc = qdoc_ref[...]

    def first_key(i):
        return pl.multiple_of(list_ref[span * spans + i] * SPAN_ROWS, SPAN_ROWS)

    for g in range(q_ref.shape[1] // DH):
        cols = slice(g * DH, (g + 1) * DH)
        q = q_ref[:, cols]
        gr = g_ref[:, cols]

        def stats(i, carry):
            m, l = carry
            start = first_key(i)
            kp = kpos_ref[:, pl.ds(start, SPAN_ROWS)]
            kd = kdoc_ref[:, pl.ds(start, SPAN_ROWS)]
            allowed = (kp <= qpos) & (kd == qdoc)
            s = lax.dot_general(
                q, k_ref[pl.ds(start, SPAN_ROWS), :], (((1,), (1,)), ((), ())),
                preferred_element_type=jnp.float32,
            ) * scale
            s = jnp.where(allowed, s, -jnp.inf)
            tiles_ref[i] = s
            m_new = jnp.maximum(m, jnp.max(s, axis=1, keepdims=True))
            l = l * jnp.exp(m - m_new) + jnp.sum(jnp.exp(s - m_new), axis=1, keepdims=True)
            return m_new, l

        m, l = lax.fori_loop(
            0, count, stats, (jnp.full((rows, 1), -1e30, jnp.float32), jnp.zeros((rows, 1), jnp.float32))
        )
        lse = m + jnp.log(l)

        def forward(i, o):
            start = first_key(i)
            p = jnp.exp(tiles_ref[i] - lse)
            tiles_ref[i] = p
            return o + jnp.dot(
                p.astype(jnp.bfloat16), v_ref[pl.ds(start, SPAN_ROWS), :], preferred_element_type=jnp.float32
            )

        o = lax.fori_loop(0, count, forward, jnp.zeros((rows, DH), jnp.float32))
        delta = jnp.sum(
            gr.astype(jnp.float32) * o.astype(jnp.bfloat16).astype(jnp.float32), axis=1, keepdims=True
        )

        def backward(i, dq):
            start = first_key(i)
            kb = k_ref[pl.ds(start, SPAN_ROWS), :]
            vb = v_ref[pl.ds(start, SPAN_ROWS), :]
            p = tiles_ref[i]
            dp = lax.dot_general(gr, vb, (((1,), (1,)), ((), ())), preferred_element_type=jnp.float32)
            ds = (p * (dp - delta)).astype(jnp.bfloat16)
            dk_ref[pl.ds(start, SPAN_ROWS), :] += lax.dot_general(
                ds, q, (((0,), (0,)), ((), ())), preferred_element_type=jnp.float32
            )
            dv_ref[pl.ds(start, SPAN_ROWS), :] += lax.dot_general(
                p.astype(jnp.bfloat16), gr, (((0,), (0,)), ((), ())), preferred_element_type=jnp.float32
            )
            return dq + jnp.dot(ds, kb, preferred_element_type=jnp.float32)

        dq = lax.fori_loop(0, count, backward, jnp.zeros((rows, DH), jnp.float32))
        dq_ref[:, cols] = dq * scale

    @pl.when(span == pl.num_programs(1) - 1)
    def _():
        dk_ref[...] = dk_ref[...] * scale


def attention(span_list, span_count, query, grad, keys, values, qpos, qdoc, kpos, kdoc, interpret=False):
    rows, width = query.shape
    keys_len, kv_width = keys.shape
    groups = width // kv_width
    heads = kv_width // DH
    q_spec = pl.BlockSpec((SPAN_ROWS, groups * DH), lambda c, s, *_: (s, c))
    k_spec = pl.BlockSpec((keys_len, DH), lambda c, s, *_: (0, c))
    col_spec = pl.BlockSpec((SPAN_ROWS, 1), lambda c, s, *_: (s, 0))
    row_spec = pl.BlockSpec((1, keys_len), lambda c, s, *_: (0, 0))
    return pl.pallas_call(
        attention_kernel,
        grid_spec=pltpu.PrefetchScalarGridSpec(
            num_scalar_prefetch=2,
            grid=(heads, rows // SPAN_ROWS),
            in_specs=[q_spec, q_spec, k_spec, k_spec, col_spec, col_spec, row_spec, row_spec],
            out_specs=[q_spec, k_spec, k_spec],
            scratch_shapes=[pltpu.VMEM((keys_len // SPAN_ROWS, SPAN_ROWS, SPAN_ROWS), jnp.float32)],
        ),
        out_shape=[
            jax.ShapeDtypeStruct((rows, width), jnp.float32),
            jax.ShapeDtypeStruct((keys_len, kv_width), jnp.float32),
            jax.ShapeDtypeStruct((keys_len, kv_width), jnp.float32),
        ],
        compiler_params=pltpu.CompilerParams(dimension_semantics=("arbitrary", "arbitrary")),
        interpret=interpret,
    )(span_list, span_count, query, grad, keys, values, qpos, qdoc, kpos, kdoc)


def visible(query_pos, query_doc, key_pos, key_doc):
    return (key_pos[None, :] <= query_pos[:, None]) & (key_doc[None, :] == query_doc[:, None])


def local(query_in, key_in, value_in, grad_out, target, span_order, doc_ids):
    local_rows = query_in.shape[0]
    devices = lax.axis_size(("dp", "ctx"))
    ctx_size = lax.axis_size("ctx")
    capacity = local_rows // devices + 2
    groups = HQ // HK
    score_scale = DH ** (-0.5)
    q_cols = query_in.shape[1]
    k_cols = key_in.shape[1]
    owners = target // local_rows
    onehot = (owners[:, None] == jnp.arange(devices, dtype=jnp.int32)[None, :]).astype(jnp.int32)
    earlier = jnp.cumsum(onehot, axis=0) - onehot
    slot_ids = owners * capacity + jnp.sum(earlier * onehot, axis=1)

    place_col = jnp.zeros((local_rows, 128), jnp.bfloat16).at[:, 0].set(
        (target % local_rows + 1).astype(jnp.bfloat16)
    )

    def exchange(payload):
        width = payload.shape[1]
        holder = jnp.zeros((devices * capacity, width), payload.dtype).at[slot_ids].set(payload)
        return lax.all_to_all(
            holder.reshape(devices, capacity, width), ("dp", "ctx"), split_axis=0, concat_axis=0, tiled=True
        ).reshape(devices * capacity, width)

    got_kv = exchange(jnp.concatenate([key_in, value_in, place_col], axis=1))
    got_qg = exchange(jnp.concatenate([query_in, grad_out], axis=1))
    arrived = got_kv[:, 2 * k_cols].astype(jnp.int32) - 1
    landing = jnp.where(arrived >= 0, arrived, local_rows)

    def unpack(values):
        return jnp.zeros((local_rows, values.shape[1]), values.dtype).at[landing].set(values, mode="drop")

    kv_rows = unpack(got_kv[:, : 2 * k_cols])
    qg_rows = unpack(got_qg)
    query = qg_rows[:, :q_cols]
    grad_rows = qg_rows[:, q_cols:]

    span_rows = local_rows // 2
    span_seq = span_order[0]
    pack_len = local_rows * ctx_size
    positions = (
        span_seq[:, None] * span_rows + jnp.arange(span_rows, dtype=jnp.int32)[None, :]
    ).reshape(-1)
    ctx_index = lax.axis_index("ctx")
    own_pos = lax.dynamic_slice_in_dim(positions, ctx_index * local_rows, local_rows)
    doc_col = jnp.zeros((local_rows, 128), jnp.bfloat16).at[:, 0].set(doc_ids[0].astype(jnp.bfloat16))
    gathered = lax.all_gather(
        jnp.concatenate([kv_rows, doc_col], axis=1), "ctx", axis=0, tiled=True
    )
    seq_docs = gathered[:, 2 * k_cols].astype(jnp.int32)
    doc_all = seq_docs.reshape(2 * ctx_size, span_rows)[span_seq].reshape(-1)
    own_docs = lax.dynamic_slice_in_dim(doc_all, ctx_index * local_rows, local_rows)
    keys_all = gathered[:, :k_cols]
    values_all = gathered[:, k_cols : 2 * k_cols]
    query_spans = local_rows // SPAN_ROWS
    key_spans = pack_len // SPAN_ROWS
    allowed_all = visible(own_pos, own_docs, positions, doc_all)
    active = jnp.any(allowed_all.reshape(query_spans, SPAN_ROWS, key_spans, SPAN_ROWS), axis=(1, 3))
    span_count = jnp.sum(active.astype(jnp.int32), axis=1)
    rank = jnp.cumsum(active.astype(jnp.int32), axis=1) - 1
    slot = jnp.where(active, rank + key_spans * jnp.arange(query_spans)[:, None], query_spans * key_spans)
    span_list = (
        jnp.zeros((query_spans * key_spans,), jnp.int32)
        .at[slot.reshape(-1)]
        .set(jnp.tile(jnp.arange(key_spans, dtype=jnp.int32), query_spans), mode="drop")
    )
    dquery_full, dkey_all, dvalue_all = attention(
        span_list,
        span_count,
        query,
        grad_rows,
        keys_all,
        values_all,
        own_pos.reshape(local_rows, 1),
        own_docs.reshape(local_rows, 1),
        positions.reshape(1, pack_len),
        doc_all.reshape(1, pack_len),
    )
    partial = jnp.concatenate([dkey_all, dvalue_all], axis=1).astype(jnp.bfloat16)
    summed_kv = jnp.sum(
        lax.all_to_all(
            partial.reshape(ctx_size, local_rows, 2 * k_cols), "ctx", split_axis=0, concat_axis=0, tiled=True
        ).astype(jnp.float32),
        axis=0,
    )
    source_rows = jnp.where(arrived >= 0, arrived, 0)
    result = jnp.concatenate([dquery_full.astype(jnp.bfloat16), summed_kv.astype(jnp.bfloat16)], axis=1)
    back = lax.all_to_all(
        result[source_rows].reshape(devices, capacity, q_cols + 2 * k_cols),
        ("dp", "ctx"),
        split_axis=0,
        concat_axis=0,
        tiled=True,
    ).reshape(devices * capacity, q_cols + 2 * k_cols)[slot_ids].astype(jnp.float32)
    return (back[:, :q_cols], back[:, q_cols : q_cols + k_cols], back[:, q_cols + k_cols :])


def solution(mesh):
    placed = (
        P(("dp", "ctx"), None),
        P(("dp", "ctx"), None),
        P(("dp", "ctx"), None),
        P(("dp", "ctx"), None),
        P(("dp", "ctx")),
        P("dp", None),
        P("dp", "ctx"),
    )
    return jax.shard_map(
        local,
        mesh=mesh,
        in_specs=placed,
        out_specs=(P(("dp", "ctx"), None), P(("dp", "ctx"), None), P(("dp", "ctx"), None)),
        check_vma=False,
    )
```

```python
import jax
import jax.numpy as jnp
from jax import lax
from jax.sharding import PartitionSpec as P
from jax.experimental import pallas as pl
from jax.experimental.pallas import tpu as pltpu

HQ = 16
HK = 4
DH = 128


SPAN_ROWS = 128


def attention_kernel(
    list_ref, count_ref, q_ref, g_ref, k_ref, v_ref, qpos_ref, qdoc_ref, kpos_ref, kdoc_ref,
    dq_ref, dk_ref, dv_ref, tiles_ref,
):
    scale = DH ** (-0.5)
    rows = q_ref.shape[0]
    heads = q_ref.shape[1] // DH
    stacked = heads * rows
    span = pl.program_id(1)
    spans = list_ref.shape[0] // pl.num_programs(1)
    count = count_ref[span]

    @pl.when(span == 0)
    def _():
        dk_ref[...] = jnp.zeros(dk_ref.shape, jnp.float32)
        dv_ref[...] = jnp.zeros(dv_ref.shape, jnp.float32)

    qpos = qpos_ref[...]
    qdoc = qdoc_ref[...]
    q = jnp.concatenate([q_ref[:, g * DH : (g + 1) * DH] for g in range(heads)], axis=0)
    gr = jnp.concatenate([g_ref[:, g * DH : (g + 1) * DH] for g in range(heads)], axis=0)

    def first_key(i):
        return pl.multiple_of(list_ref[span * spans + i] * SPAN_ROWS, SPAN_ROWS)

    def stats(i, carry):
        m, l = carry
        start = first_key(i)
        kp = kpos_ref[:, pl.ds(start, SPAN_ROWS)]
        kd = kdoc_ref[:, pl.ds(start, SPAN_ROWS)]
        allowed = (kp <= qpos) & (kd == qdoc)
        s = lax.dot_general(
            q, k_ref[pl.ds(start, SPAN_ROWS), :], (((1,), (1,)), ((), ())),
            preferred_element_type=jnp.float32,
        ) * scale
        s = jnp.where(allowed[None], s.reshape(heads, rows, SPAN_ROWS), -jnp.inf).reshape(stacked, SPAN_ROWS)
        tiles_ref[i] = s
        m_new = jnp.maximum(m, jnp.max(s, axis=1, keepdims=True))
        l = l * jnp.exp(m - m_new) + jnp.sum(jnp.exp(s - m_new), axis=1, keepdims=True)
        return m_new, l

    m, l = lax.fori_loop(
        0, count, stats, (jnp.full((stacked, 1), -1e30, jnp.float32), jnp.zeros((stacked, 1), jnp.float32))
    )
    lse = m + jnp.log(l)

    def forward(i, o):
        start = first_key(i)
        p = jnp.exp(tiles_ref[i] - lse)
        tiles_ref[i] = p
        return o + jnp.dot(
            p.astype(jnp.bfloat16), v_ref[pl.ds(start, SPAN_ROWS), :], preferred_element_type=jnp.float32
        )

    o = lax.fori_loop(0, count, forward, jnp.zeros((stacked, DH), jnp.float32))
    delta = jnp.sum(gr.astype(jnp.float32) * o.astype(jnp.bfloat16).astype(jnp.float32), axis=1, keepdims=True)

    def backward(i, dq):
        start = first_key(i)
        kb = k_ref[pl.ds(start, SPAN_ROWS), :]
        vb = v_ref[pl.ds(start, SPAN_ROWS), :]
        p = tiles_ref[i]
        dp = lax.dot_general(gr, vb, (((1,), (1,)), ((), ())), preferred_element_type=jnp.float32)
        ds = (p * (dp - delta)).astype(jnp.bfloat16)
        dk_ref[pl.ds(start, SPAN_ROWS), :] += lax.dot_general(
            ds, q, (((0,), (0,)), ((), ())), preferred_element_type=jnp.float32
        )
        dv_ref[pl.ds(start, SPAN_ROWS), :] += lax.dot_general(
            p.astype(jnp.bfloat16), gr, (((0,), (0,)), ((), ())), preferred_element_type=jnp.float32
        )
        return dq + jnp.dot(ds, kb, preferred_element_type=jnp.float32)

    dq = lax.fori_loop(0, count, backward, jnp.zeros((stacked, DH), jnp.float32)) * scale
    for g in range(heads):
        dq_ref[:, g * DH : (g + 1) * DH] = dq[g * rows : (g + 1) * rows]

    @pl.when(span == pl.num_programs(1) - 1)
    def _():
        dk_ref[...] = dk_ref[...] * scale


def attention(span_list, span_count, query, grad, keys, values, qpos, qdoc, kpos, kdoc, interpret=False):
    rows, width = query.shape
    keys_len, kv_width = keys.shape
    groups = width // kv_width
    heads = kv_width // DH
    q_spec = pl.BlockSpec((SPAN_ROWS, groups * DH), lambda c, s, *_: (s, c))
    k_spec = pl.BlockSpec((keys_len, DH), lambda c, s, *_: (0, c))
    col_spec = pl.BlockSpec((SPAN_ROWS, 1), lambda c, s, *_: (s, 0))
    row_spec = pl.BlockSpec((1, keys_len), lambda c, s, *_: (0, 0))
    return pl.pallas_call(
        attention_kernel,
        grid_spec=pltpu.PrefetchScalarGridSpec(
            num_scalar_prefetch=2,
            grid=(heads, rows // SPAN_ROWS),
            in_specs=[q_spec, q_spec, k_spec, k_spec, col_spec, col_spec, row_spec, row_spec],
            out_specs=[q_spec, k_spec, k_spec],
            scratch_shapes=[pltpu.VMEM((keys_len // SPAN_ROWS, groups * SPAN_ROWS, SPAN_ROWS), jnp.float32)],
        ),
        out_shape=[
            jax.ShapeDtypeStruct((rows, width), jnp.float32),
            jax.ShapeDtypeStruct((keys_len, kv_width), jnp.float32),
            jax.ShapeDtypeStruct((keys_len, kv_width), jnp.float32),
        ],
        compiler_params=pltpu.CompilerParams(dimension_semantics=("arbitrary", "arbitrary")),
        interpret=interpret,
    )(span_list, span_count, query, grad, keys, values, qpos, qdoc, kpos, kdoc)


def visible(query_pos, query_doc, key_pos, key_doc):
    return (key_pos[None, :] <= query_pos[:, None]) & (key_doc[None, :] == query_doc[:, None])


def local(query_in, key_in, value_in, grad_out, target, span_order, doc_ids):
    local_rows = query_in.shape[0]
    devices = lax.axis_size(("dp", "ctx"))
    ctx_size = lax.axis_size("ctx")
    capacity = local_rows // devices + 2
    groups = HQ // HK
    score_scale = DH ** (-0.5)
    q_cols = query_in.shape[1]
    k_cols = key_in.shape[1]
    owners = target // local_rows
    onehot = (owners[:, None] == jnp.arange(devices, dtype=jnp.int32)[None, :]).astype(jnp.int32)
    earlier = jnp.cumsum(onehot, axis=0) - onehot
    slot_ids = owners * capacity + jnp.sum(earlier * onehot, axis=1)

    place_col = jnp.zeros((local_rows, 128), jnp.bfloat16).at[:, 0].set(
        (target % local_rows + 1).astype(jnp.bfloat16)
    )

    def exchange(payload):
        width = payload.shape[1]
        holder = jnp.zeros((devices * capacity, width), payload.dtype).at[slot_ids].set(payload)
        return lax.all_to_all(
            holder.reshape(devices, capacity, width), ("dp", "ctx"), split_axis=0, concat_axis=0, tiled=True
        ).reshape(devices * capacity, width)

    got_kv = exchange(jnp.concatenate([key_in, value_in, place_col], axis=1))
    got_qg = exchange(jnp.concatenate([query_in, grad_out], axis=1))
    arrived = got_kv[:, 2 * k_cols].astype(jnp.int32) - 1
    landing = jnp.where(arrived >= 0, arrived, local_rows)

    def unpack(values):
        return jnp.zeros((local_rows, values.shape[1]), values.dtype).at[landing].set(values, mode="drop")

    kv_rows = unpack(got_kv[:, : 2 * k_cols])
    qg_rows = unpack(got_qg)
    query = qg_rows[:, :q_cols]
    grad_rows = qg_rows[:, q_cols:]

    span_rows = local_rows // 2
    span_seq = span_order[0]
    pack_len = local_rows * ctx_size
    positions = (
        span_seq[:, None] * span_rows + jnp.arange(span_rows, dtype=jnp.int32)[None, :]
    ).reshape(-1)
    ctx_index = lax.axis_index("ctx")
    own_pos = lax.dynamic_slice_in_dim(positions, ctx_index * local_rows, local_rows)
    doc_col = jnp.zeros((local_rows, 128), jnp.bfloat16).at[:, 0].set(doc_ids[0].astype(jnp.bfloat16))
    gathered = lax.all_gather(
        jnp.concatenate([kv_rows, doc_col], axis=1), "ctx", axis=0, tiled=True
    )
    seq_docs = gathered[:, 2 * k_cols].astype(jnp.int32)
    doc_all = seq_docs.reshape(2 * ctx_size, span_rows)[span_seq].reshape(-1)
    own_docs = lax.dynamic_slice_in_dim(doc_all, ctx_index * local_rows, local_rows)
    keys_all = gathered[:, :k_cols]
    values_all = gathered[:, k_cols : 2 * k_cols]
    query_spans = local_rows // SPAN_ROWS
    key_spans = pack_len // SPAN_ROWS
    allowed_all = visible(own_pos, own_docs, positions, doc_all)
    active = jnp.any(allowed_all.reshape(query_spans, SPAN_ROWS, key_spans, SPAN_ROWS), axis=(1, 3))
    span_count = jnp.sum(active.astype(jnp.int32), axis=1)
    rank = jnp.cumsum(active.astype(jnp.int32), axis=1) - 1
    slot = jnp.where(active, rank + key_spans * jnp.arange(query_spans)[:, None], query_spans * key_spans)
    span_list = (
        jnp.zeros((query_spans * key_spans,), jnp.int32)
        .at[slot.reshape(-1)]
        .set(jnp.tile(jnp.arange(key_spans, dtype=jnp.int32), query_spans), mode="drop")
    )
    dquery_full, dkey_all, dvalue_all = attention(
        span_list,
        span_count,
        query,
        grad_rows,
        keys_all,
        values_all,
        own_pos.reshape(local_rows, 1),
        own_docs.reshape(local_rows, 1),
        positions.reshape(1, pack_len),
        doc_all.reshape(1, pack_len),
    )
    partial = jnp.concatenate([dkey_all, dvalue_all], axis=1).astype(jnp.bfloat16)
    summed_kv = jnp.sum(
        lax.all_to_all(
            partial.reshape(ctx_size, local_rows, 2 * k_cols), "ctx", split_axis=0, concat_axis=0, tiled=True
        ).astype(jnp.float32),
        axis=0,
    )
    source_rows = jnp.where(arrived >= 0, arrived, 0)
    result = jnp.concatenate([dquery_full.astype(jnp.bfloat16), summed_kv.astype(jnp.bfloat16)], axis=1)
    back = lax.all_to_all(
        result[source_rows].reshape(devices, capacity, q_cols + 2 * k_cols),
        ("dp", "ctx"),
        split_axis=0,
        concat_axis=0,
        tiled=True,
    ).reshape(devices * capacity, q_cols + 2 * k_cols)[slot_ids].astype(jnp.float32)
    return (back[:, :q_cols], back[:, q_cols : q_cols + k_cols], back[:, q_cols + k_cols :])


def solution(mesh):
    placed = (
        P(("dp", "ctx"), None),
        P(("dp", "ctx"), None),
        P(("dp", "ctx"), None),
        P(("dp", "ctx"), None),
        P(("dp", "ctx")),
        P("dp", None),
        P("dp", "ctx"),
    )
    return jax.shard_map(
        local,
        mesh=mesh,
        in_specs=placed,
        out_specs=(P(("dp", "ctx"), None), P(("dp", "ctx"), None), P(("dp", "ctx"), None)),
        check_vma=False,
    )
```

```python
import jax
import numpy as np
import jax.numpy as jnp
from jax import lax
from jax.sharding import PartitionSpec as P
from jax.experimental import pallas as pl
from jax.experimental.pallas import tpu as pltpu

HQ = 16
HK = 4
DH = 128


SPAN_ROWS = 128


def attention_kernel(
    list_ref, count_ref, q_ref, g_ref, k_ref, v_ref, qpos_ref, qdoc_ref, kpos_ref, kdoc_ref,
    dq_ref, dk_ref, dv_ref, tiles_ref,
):
    scale = DH ** (-0.5)
    rows = q_ref.shape[0]
    heads = q_ref.shape[1] // DH
    stacked = heads * rows
    span = pl.program_id(1)
    spans = list_ref.shape[0] // pl.num_programs(1)
    count = count_ref[span]

    @pl.when(span == 0)
    def _():
        dk_ref[...] = jnp.zeros(dk_ref.shape, jnp.float32)
        dv_ref[...] = jnp.zeros(dv_ref.shape, jnp.float32)

    qpos = qpos_ref[...]
    qdoc = qdoc_ref[...]
    q = jnp.concatenate([q_ref[:, g * DH : (g + 1) * DH] for g in range(heads)], axis=0)
    gr = jnp.concatenate([g_ref[:, g * DH : (g + 1) * DH] for g in range(heads)], axis=0)

    def first_key(i):
        return pl.multiple_of(list_ref[span * spans + i] * SPAN_ROWS, SPAN_ROWS)

    def stats(i, carry):
        m, l = carry
        start = first_key(i)
        kp = kpos_ref[:, pl.ds(start, SPAN_ROWS)]
        kd = kdoc_ref[:, pl.ds(start, SPAN_ROWS)]
        allowed = (kp <= qpos) & (kd == qdoc)
        s = lax.dot_general(
            q, k_ref[pl.ds(start, SPAN_ROWS), :], (((1,), (1,)), ((), ())),
            preferred_element_type=jnp.float32,
        ) * scale
        s = jnp.where(allowed[None], s.reshape(heads, rows, SPAN_ROWS), -jnp.inf).reshape(stacked, SPAN_ROWS)
        tiles_ref[i] = s
        m_new = jnp.maximum(m, jnp.max(s, axis=1, keepdims=True))
        l = l * jnp.exp(m - m_new) + jnp.sum(jnp.exp(s - m_new), axis=1, keepdims=True)
        return m_new, l

    m, l = lax.fori_loop(
        0, count, stats, (jnp.full((stacked, 1), -1e30, jnp.float32), jnp.zeros((stacked, 1), jnp.float32))
    )
    lse = m + jnp.log(l)

    def forward(i, o):
        start = first_key(i)
        p = jnp.exp(tiles_ref[i] - lse)
        tiles_ref[i] = p
        return o + jnp.dot(
            p.astype(jnp.bfloat16), v_ref[pl.ds(start, SPAN_ROWS), :], preferred_element_type=jnp.float32
        )

    o = lax.fori_loop(0, count, forward, jnp.zeros((stacked, DH), jnp.float32))
    delta = jnp.sum(gr.astype(jnp.float32) * o.astype(jnp.bfloat16).astype(jnp.float32), axis=1, keepdims=True)

    def backward(i, dq):
        start = first_key(i)
        kb = k_ref[pl.ds(start, SPAN_ROWS), :]
        vb = v_ref[pl.ds(start, SPAN_ROWS), :]
        p = tiles_ref[i]
        dp = lax.dot_general(gr, vb, (((1,), (1,)), ((), ())), preferred_element_type=jnp.float32)
        ds = (p * (dp - delta)).astype(jnp.bfloat16)
        dk_ref[pl.ds(start, SPAN_ROWS), :] += lax.dot_general(
            ds, q, (((0,), (0,)), ((), ())), preferred_element_type=jnp.float32
        )
        dv_ref[pl.ds(start, SPAN_ROWS), :] += lax.dot_general(
            p.astype(jnp.bfloat16), gr, (((0,), (0,)), ((), ())), preferred_element_type=jnp.float32
        )
        return dq + jnp.dot(ds, kb, preferred_element_type=jnp.float32)

    dq = lax.fori_loop(0, count, backward, jnp.zeros((stacked, DH), jnp.float32)) * scale
    for g in range(heads):
        dq_ref[:, g * DH : (g + 1) * DH] = dq[g * rows : (g + 1) * rows]

    @pl.when(span == pl.num_programs(1) - 1)
    def _():
        dk_ref[...] = dk_ref[...] * scale


def attention(span_list, span_count, query, grad, keys, values, qpos, qdoc, kpos, kdoc, interpret=False):
    rows, width = query.shape
    keys_len, kv_width = keys.shape
    groups = width // kv_width
    heads = kv_width // DH
    q_spec = pl.BlockSpec((SPAN_ROWS, groups * DH), lambda c, s, *_: (s, c))
    k_spec = pl.BlockSpec((keys_len, DH), lambda c, s, *_: (0, c))
    col_spec = pl.BlockSpec((SPAN_ROWS, 1), lambda c, s, *_: (s, 0))
    row_spec = pl.BlockSpec((1, keys_len), lambda c, s, *_: (0, 0))
    return pl.pallas_call(
        attention_kernel,
        grid_spec=pltpu.PrefetchScalarGridSpec(
            num_scalar_prefetch=2,
            grid=(heads, rows // SPAN_ROWS),
            in_specs=[q_spec, q_spec, k_spec, k_spec, col_spec, col_spec, row_spec, row_spec],
            out_specs=[q_spec, k_spec, k_spec],
            scratch_shapes=[pltpu.VMEM((keys_len // SPAN_ROWS, groups * SPAN_ROWS, SPAN_ROWS), jnp.float32)],
        ),
        out_shape=[
            jax.ShapeDtypeStruct((rows, width), jnp.float32),
            jax.ShapeDtypeStruct((keys_len, kv_width), jnp.float32),
            jax.ShapeDtypeStruct((keys_len, kv_width), jnp.float32),
        ],
        compiler_params=pltpu.CompilerParams(dimension_semantics=("arbitrary", "arbitrary")),
        interpret=interpret,
    )(span_list, span_count, query, grad, keys, values, qpos, qdoc, kpos, kdoc)


def visible(query_pos, query_doc, key_pos, key_doc):
    return (key_pos[None, :] <= query_pos[:, None]) & (key_doc[None, :] == query_doc[:, None])


def local(query_in, key_in, value_in, grad_out, target, span_order, doc_ids):
    local_rows = query_in.shape[0]
    devices = lax.axis_size(("dp", "ctx"))
    ctx_size = lax.axis_size("ctx")
    packs = devices // ctx_size
    pack_len = local_rows * ctx_size
    capacity = (local_rows // devices + 2) * ctx_size
    q_cols = query_in.shape[1]
    k_cols = key_in.shape[1]
    q_width = q_cols // ctx_size
    k_width = k_cols // ctx_size
    ctx_ids = np.arange(ctx_size)
    kv_of = (ctx_ids // 4) * 2 + ctx_ids % 2
    half_of = (ctx_ids // 2) % 2
    block_of = 2 * kv_of + half_of
    ctx_of_block = np.argsort(block_of)

    pack_of = target // pack_len
    row_in_pack = target % pack_len
    onehot = (pack_of[:, None] == jnp.arange(packs, dtype=jnp.int32)[None, :]).astype(jnp.int32)
    slot = jnp.sum((jnp.cumsum(onehot, axis=0) - onehot) * onehot, axis=1)
    dest_pack = pack_of[:, None]
    dest_ctx = jnp.asarray(ctx_ids, jnp.int32)[None, :]
    dest_slot = slot[:, None]

    payload = jnp.concatenate(
        [
            query_in.reshape(local_rows, ctx_size, q_width)[:, block_of],
            grad_out.reshape(local_rows, ctx_size, q_width)[:, block_of],
            key_in.reshape(local_rows, k_cols // DH, DH)[:, kv_of],
            value_in.reshape(local_rows, k_cols // DH, DH)[:, kv_of],
        ],
        axis=2,
    )
    width = payload.shape[2]
    holder = (
        jnp.zeros((packs, ctx_size, capacity, width), jnp.bfloat16)
        .at[dest_pack, dest_ctx, dest_slot]
        .set(payload)
        .reshape(devices * capacity, width)
    )
    places = (
        jnp.zeros((packs, ctx_size, capacity), jnp.int32)
        .at[dest_pack, dest_ctx, dest_slot]
        .set(jnp.broadcast_to((row_in_pack + 1)[:, None], (local_rows, ctx_size)))
        .reshape(devices * capacity)
    )
    got = lax.all_to_all(holder, ("dp", "ctx"), split_axis=0, concat_axis=0, tiled=True)
    got_places = lax.all_to_all(places, ("dp", "ctx"), split_axis=0, concat_axis=0, tiled=True)
    landing = jnp.where(got_places > 0, got_places - 1, pack_len)
    rows = jnp.zeros((pack_len, width), jnp.bfloat16).at[landing].set(got, mode="drop")
    query = rows[:, :q_width]
    grad_rows = rows[:, q_width : 2 * q_width]
    keys = rows[:, 2 * q_width : 2 * q_width + DH]
    values = rows[:, 2 * q_width + DH : 2 * q_width + 2 * DH]

    span_seq = span_order[0]
    span_rows = pack_len // span_seq.shape[0]
    positions = (
        span_seq[:, None] * span_rows + jnp.arange(span_rows, dtype=jnp.int32)[None, :]
    ).reshape(-1)
    seq_docs = lax.all_gather(doc_ids[0], "ctx", axis=0, tiled=True)
    doc_all = seq_docs[positions]

    spans = pack_len // SPAN_ROWS
    allowed_all = visible(positions, doc_all, positions, doc_all)
    active = jnp.any(allowed_all.reshape(spans, SPAN_ROWS, spans, SPAN_ROWS), axis=(1, 3))
    span_count = jnp.sum(active.astype(jnp.int32), axis=1)
    rank = jnp.cumsum(active.astype(jnp.int32), axis=1) - 1
    slot_of = jnp.where(active, rank + spans * jnp.arange(spans)[:, None], spans * spans)
    span_list = (
        jnp.zeros((spans * spans,), jnp.int32)
        .at[slot_of.reshape(-1)]
        .set(jnp.tile(jnp.arange(spans, dtype=jnp.int32), spans), mode="drop")
    )
    dquery, dkey, dvalue = attention(
        span_list,
        span_count,
        query,
        grad_rows,
        keys,
        values,
        positions.reshape(pack_len, 1),
        doc_all.reshape(pack_len, 1),
        positions.reshape(1, pack_len),
        doc_all.reshape(1, pack_len),
    )

    half = jnp.asarray(half_of, jnp.int32)[lax.axis_index("ctx")]
    split_key = dkey.reshape(pack_len, 2, k_width)
    split_value = dvalue.reshape(pack_len, 2, k_width)
    mine = jnp.concatenate(
        [lax.dynamic_index_in_dim(split_key, half, 1, False), lax.dynamic_index_in_dim(split_value, half, 1, False)],
        axis=1,
    )
    other = jnp.concatenate(
        [
            lax.dynamic_index_in_dim(split_key, 1 - half, 1, False),
            lax.dynamic_index_in_dim(split_value, 1 - half, 1, False),
        ],
        axis=1,
    ).astype(jnp.bfloat16)
    partner = [(int(c), int(c) ^ 2) for c in ctx_ids]
    key_value = mine + lax.ppermute(other, "ctx", partner).astype(jnp.float32)

    result = jnp.concatenate([dquery.astype(jnp.bfloat16), key_value.astype(jnp.bfloat16)], axis=1)
    source_rows = jnp.where(landing < pack_len, landing, 0)
    back = lax.all_to_all(
        result[source_rows], ("dp", "ctx"), split_axis=0, concat_axis=0, tiled=True
    ).reshape(packs, ctx_size, capacity, result.shape[1])
    pieces = back[dest_pack, jnp.asarray(ctx_of_block, jnp.int32)[None, :], dest_slot].astype(jnp.float32)
    return (
        pieces[:, :, :q_width].reshape(local_rows, q_cols),
        pieces[:, :, q_width : q_width + k_width].reshape(local_rows, k_cols),
        pieces[:, :, q_width + k_width :].reshape(local_rows, k_cols),
    )


def solution(mesh):
    placed = (
        P(("dp", "ctx"), None),
        P(("dp", "ctx"), None),
        P(("dp", "ctx"), None),
        P(("dp", "ctx"), None),
        P(("dp", "ctx")),
        P("dp", None),
        P("dp", "ctx"),
    )
    return jax.shard_map(
        local,
        mesh=mesh,
        in_specs=placed,
        out_specs=(P(("dp", "ctx"), None), P(("dp", "ctx"), None), P(("dp", "ctx"), None)),
        check_vma=False,
    )
```

```python
import jax
import numpy as np
import jax.numpy as jnp
from jax import lax
from jax.sharding import PartitionSpec as P
from jax.experimental import pallas as pl
from jax.experimental.pallas import tpu as pltpu

HQ = 16
HK = 4
DH = 128


SPAN_ROWS = 128


def attention_kernel(
    list_ref, count_ref, q_ref, g_ref, k_ref, v_ref, qpos_ref, qdoc_ref, kpos_ref, kdoc_ref,
    dq_ref, dk_ref, dv_ref, tiles_ref,
):
    scale = DH ** (-0.5)
    rows = q_ref.shape[0]
    heads = q_ref.shape[1] // DH
    stacked = heads * rows
    span = pl.program_id(1)
    spans = list_ref.shape[0] // pl.num_programs(1)
    count = count_ref[span]

    @pl.when(span == 0)
    def _():
        dk_ref[...] = jnp.zeros(dk_ref.shape, jnp.float32)
        dv_ref[...] = jnp.zeros(dv_ref.shape, jnp.float32)

    qpos = qpos_ref[...]
    qdoc = qdoc_ref[...]
    q = jnp.concatenate([q_ref[:, g * DH : (g + 1) * DH] for g in range(heads)], axis=0)
    gr = jnp.concatenate([g_ref[:, g * DH : (g + 1) * DH] for g in range(heads)], axis=0)

    def first_key(i):
        return pl.multiple_of(list_ref[span * spans + i] * SPAN_ROWS, SPAN_ROWS)

    def stats(i, carry):
        m, l = carry
        start = first_key(i)
        kp = kpos_ref[:, pl.ds(start, SPAN_ROWS)]
        kd = kdoc_ref[:, pl.ds(start, SPAN_ROWS)]
        allowed = (kp <= qpos) & (kd == qdoc)
        s = lax.dot_general(
            q, k_ref[pl.ds(start, SPAN_ROWS), :], (((1,), (1,)), ((), ())),
            preferred_element_type=jnp.float32,
        ) * scale
        s = jnp.where(allowed[None], s.reshape(heads, rows, SPAN_ROWS), -jnp.inf).reshape(stacked, SPAN_ROWS)
        tiles_ref[i] = s
        m_new = jnp.maximum(m, jnp.max(s, axis=1, keepdims=True))
        l = l * jnp.exp(m - m_new) + jnp.sum(jnp.exp(s - m_new), axis=1, keepdims=True)
        return m_new, l

    m, l = lax.fori_loop(
        0, count, stats, (jnp.full((stacked, 1), -1e30, jnp.float32), jnp.zeros((stacked, 1), jnp.float32))
    )
    lse = m + jnp.log(l)

    def forward(i, o):
        start = first_key(i)
        p = jnp.exp(tiles_ref[i] - lse)
        tiles_ref[i] = p
        return o + jnp.dot(
            p.astype(jnp.bfloat16), v_ref[pl.ds(start, SPAN_ROWS), :], preferred_element_type=jnp.float32
        )

    o = lax.fori_loop(0, count, forward, jnp.zeros((stacked, DH), jnp.float32))
    delta = jnp.sum(gr.astype(jnp.float32) * o.astype(jnp.bfloat16).astype(jnp.float32), axis=1, keepdims=True)

    def backward(i, dq):
        start = first_key(i)
        kb = k_ref[pl.ds(start, SPAN_ROWS), :]
        vb = v_ref[pl.ds(start, SPAN_ROWS), :]
        p = tiles_ref[i]
        dp = lax.dot_general(gr, vb, (((1,), (1,)), ((), ())), preferred_element_type=jnp.float32)
        ds = (p * (dp - delta)).astype(jnp.bfloat16)
        dk_ref[pl.ds(start, SPAN_ROWS), :] += lax.dot_general(
            ds, q, (((0,), (0,)), ((), ())), preferred_element_type=jnp.float32
        )
        dv_ref[pl.ds(start, SPAN_ROWS), :] += lax.dot_general(
            p.astype(jnp.bfloat16), gr, (((0,), (0,)), ((), ())), preferred_element_type=jnp.float32
        )
        return dq + jnp.dot(ds, kb, preferred_element_type=jnp.float32)

    dq = lax.fori_loop(0, count, backward, jnp.zeros((stacked, DH), jnp.float32)) * scale
    for g in range(heads):
        dq_ref[:, g * DH : (g + 1) * DH] = dq[g * rows : (g + 1) * rows]

    @pl.when(span == pl.num_programs(1) - 1)
    def _():
        dk_ref[...] = dk_ref[...] * scale


def attention(span_list, span_count, query, grad, keys, values, qpos, qdoc, kpos, kdoc, interpret=False):
    rows, width = query.shape
    keys_len, kv_width = keys.shape
    groups = width // kv_width
    heads = kv_width // DH
    q_spec = pl.BlockSpec((SPAN_ROWS, groups * DH), lambda c, s, *_: (s, c))
    k_spec = pl.BlockSpec((keys_len, DH), lambda c, s, *_: (0, c))
    col_spec = pl.BlockSpec((SPAN_ROWS, 1), lambda c, s, *_: (s, 0))
    row_spec = pl.BlockSpec((1, keys_len), lambda c, s, *_: (0, 0))
    return pl.pallas_call(
        attention_kernel,
        grid_spec=pltpu.PrefetchScalarGridSpec(
            num_scalar_prefetch=2,
            grid=(heads, rows // SPAN_ROWS),
            in_specs=[q_spec, q_spec, k_spec, k_spec, col_spec, col_spec, row_spec, row_spec],
            out_specs=[q_spec, k_spec, k_spec],
            scratch_shapes=[pltpu.VMEM((keys_len // SPAN_ROWS, groups * SPAN_ROWS, SPAN_ROWS), jnp.float32)],
        ),
        out_shape=[
            jax.ShapeDtypeStruct((rows, width), jnp.float32),
            jax.ShapeDtypeStruct((keys_len, kv_width), jnp.float32),
            jax.ShapeDtypeStruct((keys_len, kv_width), jnp.float32),
        ],
        compiler_params=pltpu.CompilerParams(dimension_semantics=("arbitrary", "arbitrary")),
        interpret=interpret,
    )(span_list, span_count, query, grad, keys, values, qpos, qdoc, kpos, kdoc)


def visible(query_pos, query_doc, key_pos, key_doc):
    return (key_pos[None, :] <= query_pos[:, None]) & (key_doc[None, :] == query_doc[:, None])


def local(query_in, key_in, value_in, grad_out, target, span_order, doc_ids):
    local_rows = query_in.shape[0]
    devices = lax.axis_size(("dp", "ctx"))
    ctx_size = lax.axis_size("ctx")
    packs = devices // ctx_size
    pack_len = local_rows * ctx_size
    capacity = (local_rows // devices + 2) * ctx_size
    q_cols = query_in.shape[1]
    k_cols = key_in.shape[1]
    q_width = q_cols // ctx_size
    k_width = k_cols // ctx_size
    ctx_ids = np.arange(ctx_size)
    kv_of = (ctx_ids // 4) * 2 + ctx_ids % 2
    half_of = (ctx_ids // 2) % 2
    block_of = 2 * kv_of + half_of
    ctx_of_block = np.argsort(block_of)

    pack_of = target // pack_len
    row_in_pack = target % pack_len
    onehot = (pack_of[:, None] == jnp.arange(packs, dtype=jnp.int32)[None, :]).astype(jnp.int32)
    slot = jnp.sum((jnp.cumsum(onehot, axis=0) - onehot) * onehot, axis=1)
    dest_pack = pack_of[:, None]
    dest_ctx = jnp.asarray(ctx_ids, jnp.int32)[None, :]
    dest_slot = slot[:, None]

    payload = jnp.concatenate(
        [
            query_in.reshape(local_rows, ctx_size, q_width)[:, block_of],
            grad_out.reshape(local_rows, ctx_size, q_width)[:, block_of],
            key_in.reshape(local_rows, k_cols // DH, DH)[:, kv_of],
            value_in.reshape(local_rows, k_cols // DH, DH)[:, kv_of],
        ],
        axis=2,
    )
    width = payload.shape[2]
    flat_slot = pack_of * capacity + slot
    holder = (
        jnp.zeros((packs * capacity, ctx_size * width), jnp.bfloat16)
        .at[flat_slot]
        .set(payload.reshape(local_rows, ctx_size * width))
        .reshape(packs, capacity, ctx_size, width)
        .transpose(0, 2, 1, 3)
        .reshape(devices * capacity, width)
    )
    places = jnp.broadcast_to(
        jnp.zeros((packs, 1, capacity), jnp.int32)
        .at[pack_of, 0, slot]
        .set(row_in_pack + 1),
        (packs, ctx_size, capacity),
    ).reshape(devices * capacity)
    got = lax.all_to_all(holder, ("dp", "ctx"), split_axis=0, concat_axis=0, tiled=True)
    got_places = lax.all_to_all(places, ("dp", "ctx"), split_axis=0, concat_axis=0, tiled=True)
    landing = jnp.where(got_places > 0, got_places - 1, pack_len)
    rows = jnp.zeros((pack_len, width), jnp.bfloat16).at[landing].set(got, mode="drop")
    query = rows[:, :q_width]
    grad_rows = rows[:, q_width : 2 * q_width]
    keys = rows[:, 2 * q_width : 2 * q_width + DH]
    values = rows[:, 2 * q_width + DH : 2 * q_width + 2 * DH]

    span_seq = span_order[0]
    span_rows = pack_len // span_seq.shape[0]
    positions = (
        span_seq[:, None] * span_rows + jnp.arange(span_rows, dtype=jnp.int32)[None, :]
    ).reshape(-1)
    seq_docs = lax.all_gather(doc_ids[0], "ctx", axis=0, tiled=True)
    span_docs = seq_docs.reshape(span_seq.shape[0], span_rows)[span_seq]
    doc_all = span_docs.reshape(-1)

    spans = pack_len // SPAN_ROWS
    first_doc = span_docs[:, 0]
    last_doc = span_docs[:, -1]
    active = (
        (span_seq[None, :] <= span_seq[:, None])
        & (first_doc[None, :] <= last_doc[:, None])
        & (first_doc[:, None] <= last_doc[None, :])
    )
    span_count = jnp.sum(active.astype(jnp.int32), axis=1)
    rank = jnp.cumsum(active.astype(jnp.int32), axis=1) - 1
    slot_of = jnp.where(active, rank + spans * jnp.arange(spans)[:, None], spans * spans)
    span_list = (
        jnp.zeros((spans * spans,), jnp.int32)
        .at[slot_of.reshape(-1)]
        .set(jnp.tile(jnp.arange(spans, dtype=jnp.int32), spans), mode="drop")
    )
    dquery, dkey, dvalue = attention(
        span_list,
        span_count,
        query,
        grad_rows,
        keys,
        values,
        positions.reshape(pack_len, 1),
        doc_all.reshape(pack_len, 1),
        positions.reshape(1, pack_len),
        doc_all.reshape(1, pack_len),
    )

    half = jnp.asarray(half_of, jnp.int32)[lax.axis_index("ctx")]
    split_key = dkey.reshape(pack_len, 2, k_width)
    split_value = dvalue.reshape(pack_len, 2, k_width)
    mine = jnp.concatenate(
        [lax.dynamic_index_in_dim(split_key, half, 1, False), lax.dynamic_index_in_dim(split_value, half, 1, False)],
        axis=1,
    )
    other = jnp.concatenate(
        [
            lax.dynamic_index_in_dim(split_key, 1 - half, 1, False),
            lax.dynamic_index_in_dim(split_value, 1 - half, 1, False),
        ],
        axis=1,
    ).astype(jnp.bfloat16)
    partner = [(int(c), int(c) ^ 2) for c in ctx_ids]
    key_value = mine + lax.ppermute(other, "ctx", partner).astype(jnp.float32)

    result = jnp.concatenate([dquery.astype(jnp.bfloat16), key_value.astype(jnp.bfloat16)], axis=1)
    source_rows = jnp.where(landing < pack_len, landing, 0)
    back = (
        lax.all_to_all(result[source_rows], ("dp", "ctx"), split_axis=0, concat_axis=0, tiled=True)
        .reshape(packs, ctx_size, capacity, result.shape[1])
        .transpose(0, 2, 1, 3)
        .reshape(packs * capacity, ctx_size, result.shape[1])
    )
    pieces = back[flat_slot][:, ctx_of_block].astype(jnp.float32)
    return (
        pieces[:, :, :q_width].reshape(local_rows, q_cols),
        pieces[:, :, q_width : q_width + k_width].reshape(local_rows, k_cols),
        pieces[:, :, q_width + k_width :].reshape(local_rows, k_cols),
    )


def solution(mesh):
    placed = (
        P(("dp", "ctx"), None),
        P(("dp", "ctx"), None),
        P(("dp", "ctx"), None),
        P(("dp", "ctx"), None),
        P(("dp", "ctx")),
        P("dp", None),
        P("dp", "ctx"),
    )
    return jax.shard_map(
        local,
        mesh=mesh,
        in_specs=placed,
        out_specs=(P(("dp", "ctx"), None), P(("dp", "ctx"), None), P(("dp", "ctx"), None)),
        check_vma=False,
    )
```

```python
import jax
import numpy as np
import jax.numpy as jnp
from jax import lax
from jax.sharding import PartitionSpec as P
from jax.experimental import pallas as pl
from jax.experimental.pallas import tpu as pltpu

HQ = 16
HK = 4
DH = 128


SPAN_ROWS = 256


def attention_kernel(
    list_ref, count_ref, q_ref, g_ref, k_ref, v_ref, qpos_ref, qdoc_ref, kpos_ref, kdoc_ref,
    dq_ref, dk_ref, dv_ref, tiles_ref,
):
    scale = DH ** (-0.5)
    rows = q_ref.shape[0]
    heads = q_ref.shape[1] // DH
    stacked = heads * rows
    span = pl.program_id(1)
    spans = list_ref.shape[0] // pl.num_programs(1)
    count = count_ref[span]

    @pl.when(span == 0)
    def _():
        dk_ref[...] = jnp.zeros(dk_ref.shape, jnp.float32)
        dv_ref[...] = jnp.zeros(dv_ref.shape, jnp.float32)

    qpos = qpos_ref[...]
    qdoc = qdoc_ref[...]
    q = jnp.concatenate([q_ref[:, g * DH : (g + 1) * DH] for g in range(heads)], axis=0)
    gr = jnp.concatenate([g_ref[:, g * DH : (g + 1) * DH] for g in range(heads)], axis=0)

    def first_key(i):
        return pl.multiple_of(list_ref[span * spans + i] * SPAN_ROWS, SPAN_ROWS)

    def stats(i, carry):
        m, l = carry
        start = first_key(i)
        kp = kpos_ref[:, pl.ds(start, SPAN_ROWS)]
        kd = kdoc_ref[:, pl.ds(start, SPAN_ROWS)]
        allowed = (kp <= qpos) & (kd == qdoc)
        s = lax.dot_general(
            q, k_ref[pl.ds(start, SPAN_ROWS), :], (((1,), (1,)), ((), ())),
            preferred_element_type=jnp.float32,
        ) * scale
        s = jnp.where(allowed[None], s.reshape(heads, rows, SPAN_ROWS), -jnp.inf).reshape(stacked, SPAN_ROWS)
        tiles_ref[i] = s
        m_new = jnp.maximum(m, jnp.max(s, axis=1, keepdims=True))
        l = l * jnp.exp(m - m_new) + jnp.sum(jnp.exp(s - m_new), axis=1, keepdims=True)
        return m_new, l

    m, l = lax.fori_loop(
        0, count, stats, (jnp.full((stacked, 1), -1e30, jnp.float32), jnp.zeros((stacked, 1), jnp.float32))
    )
    lse = m + jnp.log(l)

    def forward(i, o):
        start = first_key(i)
        p = jnp.exp(tiles_ref[i] - lse)
        tiles_ref[i] = p
        return o + jnp.dot(
            p.astype(jnp.bfloat16), v_ref[pl.ds(start, SPAN_ROWS), :], preferred_element_type=jnp.float32
        )

    o = lax.fori_loop(0, count, forward, jnp.zeros((stacked, DH), jnp.float32))
    delta = jnp.sum(gr.astype(jnp.float32) * o.astype(jnp.bfloat16).astype(jnp.float32), axis=1, keepdims=True)

    def backward(i, dq):
        start = first_key(i)
        kb = k_ref[pl.ds(start, SPAN_ROWS), :]
        vb = v_ref[pl.ds(start, SPAN_ROWS), :]
        p = tiles_ref[i]
        dp = lax.dot_general(gr, vb, (((1,), (1,)), ((), ())), preferred_element_type=jnp.float32)
        ds = (p * (dp - delta)).astype(jnp.bfloat16)
        dk_ref[pl.ds(start, SPAN_ROWS), :] += lax.dot_general(
            ds, q, (((0,), (0,)), ((), ())), preferred_element_type=jnp.float32
        )
        dv_ref[pl.ds(start, SPAN_ROWS), :] += lax.dot_general(
            p.astype(jnp.bfloat16), gr, (((0,), (0,)), ((), ())), preferred_element_type=jnp.float32
        )
        return dq + jnp.dot(ds, kb, preferred_element_type=jnp.float32)

    dq = lax.fori_loop(0, count, backward, jnp.zeros((stacked, DH), jnp.float32)) * scale
    for g in range(heads):
        dq_ref[:, g * DH : (g + 1) * DH] = dq[g * rows : (g + 1) * rows]

    @pl.when(span == pl.num_programs(1) - 1)
    def _():
        dk_ref[...] = dk_ref[...] * scale


def attention(span_list, span_count, query, grad, keys, values, qpos, qdoc, kpos, kdoc, interpret=False):
    rows, width = query.shape
    keys_len, kv_width = keys.shape
    groups = width // kv_width
    heads = kv_width // DH
    q_spec = pl.BlockSpec((SPAN_ROWS, groups * DH), lambda c, s, *_: (s, c))
    k_spec = pl.BlockSpec((keys_len, DH), lambda c, s, *_: (0, c))
    col_spec = pl.BlockSpec((SPAN_ROWS, 1), lambda c, s, *_: (s, 0))
    row_spec = pl.BlockSpec((1, keys_len), lambda c, s, *_: (0, 0))
    return pl.pallas_call(
        attention_kernel,
        grid_spec=pltpu.PrefetchScalarGridSpec(
            num_scalar_prefetch=2,
            grid=(heads, rows // SPAN_ROWS),
            in_specs=[q_spec, q_spec, k_spec, k_spec, col_spec, col_spec, row_spec, row_spec],
            out_specs=[q_spec, k_spec, k_spec],
            scratch_shapes=[pltpu.VMEM((keys_len // SPAN_ROWS, groups * SPAN_ROWS, SPAN_ROWS), jnp.float32)],
        ),
        out_shape=[
            jax.ShapeDtypeStruct((rows, width), jnp.float32),
            jax.ShapeDtypeStruct((keys_len, kv_width), jnp.float32),
            jax.ShapeDtypeStruct((keys_len, kv_width), jnp.float32),
        ],
        compiler_params=pltpu.CompilerParams(dimension_semantics=("arbitrary", "arbitrary")),
        interpret=interpret,
    )(span_list, span_count, query, grad, keys, values, qpos, qdoc, kpos, kdoc)


def visible(query_pos, query_doc, key_pos, key_doc):
    return (key_pos[None, :] <= query_pos[:, None]) & (key_doc[None, :] == query_doc[:, None])


def local(query_in, key_in, value_in, grad_out, target, span_order, doc_ids):
    local_rows = query_in.shape[0]
    devices = lax.axis_size(("dp", "ctx"))
    ctx_size = lax.axis_size("ctx")
    packs = devices // ctx_size
    pack_len = local_rows * ctx_size
    capacity = (local_rows // devices + 2) * ctx_size
    q_cols = query_in.shape[1]
    k_cols = key_in.shape[1]
    q_width = q_cols // ctx_size
    k_width = k_cols // ctx_size
    ctx_ids = np.arange(ctx_size)
    kv_of = (ctx_ids // 4) * 2 + ctx_ids % 2
    half_of = (ctx_ids // 2) % 2
    block_of = 2 * kv_of + half_of
    ctx_of_block = np.argsort(block_of)

    pack_of = target // pack_len
    row_in_pack = target % pack_len
    onehot = (pack_of[:, None] == jnp.arange(packs, dtype=jnp.int32)[None, :]).astype(jnp.int32)
    slot = jnp.sum((jnp.cumsum(onehot, axis=0) - onehot) * onehot, axis=1)
    dest_pack = pack_of[:, None]
    dest_ctx = jnp.asarray(ctx_ids, jnp.int32)[None, :]
    dest_slot = slot[:, None]

    payload = jnp.concatenate(
        [
            query_in.reshape(local_rows, ctx_size, q_width)[:, block_of],
            grad_out.reshape(local_rows, ctx_size, q_width)[:, block_of],
            key_in.reshape(local_rows, k_cols // DH, DH)[:, kv_of],
            value_in.reshape(local_rows, k_cols // DH, DH)[:, kv_of],
        ],
        axis=2,
    )
    width = payload.shape[2]
    flat_slot = pack_of * capacity + slot
    holder = (
        jnp.zeros((packs * capacity, ctx_size * width), jnp.bfloat16)
        .at[flat_slot]
        .set(payload.reshape(local_rows, ctx_size * width))
        .reshape(packs, capacity, ctx_size, width)
        .transpose(0, 2, 1, 3)
        .reshape(devices * capacity, width)
    )
    places = jnp.broadcast_to(
        jnp.zeros((packs, 1, capacity), jnp.int32)
        .at[pack_of, 0, slot]
        .set(row_in_pack + 1),
        (packs, ctx_size, capacity),
    ).reshape(devices * capacity)
    got = lax.all_to_all(holder, ("dp", "ctx"), split_axis=0, concat_axis=0, tiled=True)
    got_places = lax.all_to_all(places, ("dp", "ctx"), split_axis=0, concat_axis=0, tiled=True)
    span_seq = span_order[0]
    span_rows = pack_len // span_seq.shape[0]
    slot_pos = jnp.concatenate(
        [
            (span_seq[:, None] * span_rows + jnp.arange(span_rows, dtype=jnp.int32)[None, :]).reshape(-1),
            jnp.full((1,), pack_len, jnp.int32),
        ]
    )
    landing = slot_pos[jnp.where(got_places > 0, got_places - 1, pack_len)]
    rows = jnp.zeros((pack_len, width), jnp.bfloat16).at[landing].set(got, mode="drop")
    query = rows[:, :q_width]
    grad_rows = rows[:, q_width : 2 * q_width]
    keys = rows[:, 2 * q_width : 2 * q_width + DH]
    values = rows[:, 2 * q_width + DH : 2 * q_width + 2 * DH]

    doc_block = jnp.broadcast_to(doc_ids[0].astype(jnp.bfloat16)[:, None], (local_rows, 128))
    doc_all = lax.all_gather(doc_block, "ctx", axis=0, tiled=True)[:, 0].astype(jnp.int32)
    positions = jnp.arange(pack_len, dtype=jnp.int32)

    spans = pack_len // SPAN_ROWS
    tile_docs = doc_all.reshape(spans, SPAN_ROWS)
    first_doc = tile_docs[:, 0]
    last_doc = tile_docs[:, -1]
    tile_ids = jnp.arange(spans)
    active = (
        (tile_ids[None, :] <= tile_ids[:, None])
        & (first_doc[None, :] <= last_doc[:, None])
        & (first_doc[:, None] <= last_doc[None, :])
    )
    span_count = jnp.sum(active.astype(jnp.int32), axis=1)
    rank = jnp.cumsum(active.astype(jnp.int32), axis=1) - 1
    slot_of = jnp.where(active, rank + spans * jnp.arange(spans)[:, None], spans * spans)
    span_list = (
        jnp.zeros((spans * spans,), jnp.int32)
        .at[slot_of.reshape(-1)]
        .set(jnp.tile(jnp.arange(spans, dtype=jnp.int32), spans), mode="drop")
    )
    dquery, dkey, dvalue = attention(
        span_list,
        span_count,
        query,
        grad_rows,
        keys,
        values,
        positions.reshape(pack_len, 1),
        doc_all.reshape(pack_len, 1),
        positions.reshape(1, pack_len),
        doc_all.reshape(1, pack_len),
    )

    half = jnp.asarray(half_of, jnp.int32)[lax.axis_index("ctx")]
    split_key = dkey.reshape(pack_len, 2, k_width)
    split_value = dvalue.reshape(pack_len, 2, k_width)
    mine = jnp.concatenate(
        [lax.dynamic_index_in_dim(split_key, half, 1, False), lax.dynamic_index_in_dim(split_value, half, 1, False)],
        axis=1,
    )
    other = jnp.concatenate(
        [
            lax.dynamic_index_in_dim(split_key, 1 - half, 1, False),
            lax.dynamic_index_in_dim(split_value, 1 - half, 1, False),
        ],
        axis=1,
    ).astype(jnp.bfloat16)
    partner = [(int(c), int(c) ^ 2) for c in ctx_ids]
    key_value = mine + lax.ppermute(other, "ctx", partner).astype(jnp.float32)

    result = jnp.concatenate([dquery.astype(jnp.bfloat16), key_value.astype(jnp.bfloat16)], axis=1)
    source_rows = jnp.where(landing < pack_len, landing, 0)
    back = (
        lax.all_to_all(result[source_rows], ("dp", "ctx"), split_axis=0, concat_axis=0, tiled=True)
        .reshape(packs, ctx_size, capacity, result.shape[1])
        .transpose(0, 2, 1, 3)
        .reshape(packs * capacity, ctx_size, result.shape[1])
    )
    pieces = back[flat_slot][:, ctx_of_block].astype(jnp.float32)
    return (
        pieces[:, :, :q_width].reshape(local_rows, q_cols),
        pieces[:, :, q_width : q_width + k_width].reshape(local_rows, k_cols),
        pieces[:, :, q_width + k_width :].reshape(local_rows, k_cols),
    )


def solution(mesh):
    placed = (
        P(("dp", "ctx"), None),
        P(("dp", "ctx"), None),
        P(("dp", "ctx"), None),
        P(("dp", "ctx"), None),
        P(("dp", "ctx")),
        P("dp", None),
        P("dp", "ctx"),
    )
    return jax.shard_map(
        local,
        mesh=mesh,
        in_specs=placed,
        out_specs=(P(("dp", "ctx"), None), P(("dp", "ctx"), None), P(("dp", "ctx"), None)),
        check_vma=False,
    )
```

```python
import jax
import numpy as np
import jax.numpy as jnp
from jax import lax
from jax.sharding import PartitionSpec as P
from jax.experimental import pallas as pl
from jax.experimental.pallas import tpu as pltpu

HQ = 16
HK = 4
DH = 128


SPAN_ROWS = 256


def attention_kernel(
    list_ref, count_ref, q_ref, g_ref, k_ref, v_ref, qpos_ref, qdoc_ref, kpos_ref, kdoc_ref,
    dq_ref, dk_ref, dv_ref, tiles_ref,
):
    scale = DH ** (-0.5)
    rows = q_ref.shape[0]
    heads = q_ref.shape[1] // DH
    stacked = heads * rows
    span = pl.program_id(1)
    spans = list_ref.shape[0] // pl.num_programs(1)
    count = count_ref[span]

    @pl.when(span == 0)
    def _():
        dk_ref[...] = jnp.zeros(dk_ref.shape, jnp.float32)
        dv_ref[...] = jnp.zeros(dv_ref.shape, jnp.float32)

    qpos = qpos_ref[...]
    qdoc = qdoc_ref[...]
    q = jnp.concatenate([q_ref[:, g * DH : (g + 1) * DH] for g in range(heads)], axis=0)
    gr = jnp.concatenate([g_ref[:, g * DH : (g + 1) * DH] for g in range(heads)], axis=0)

    def first_key(i):
        return pl.multiple_of(list_ref[span * spans + i] * SPAN_ROWS, SPAN_ROWS)

    def stats(i, carry):
        m, l = carry
        start = first_key(i)
        kp = kpos_ref[:, pl.ds(start, SPAN_ROWS)]
        kd = kdoc_ref[:, pl.ds(start, SPAN_ROWS)]
        allowed = (kp <= qpos) & (kd == qdoc)
        s = lax.dot_general(
            q, k_ref[pl.ds(start, SPAN_ROWS), :], (((1,), (1,)), ((), ())),
            preferred_element_type=jnp.float32,
        ) * scale
        s = jnp.where(allowed[None], s.reshape(heads, rows, SPAN_ROWS), -jnp.inf).reshape(stacked, SPAN_ROWS)
        tiles_ref[i] = s
        m_new = jnp.maximum(m, jnp.max(s, axis=1, keepdims=True))
        l = l * jnp.exp(m - m_new) + jnp.sum(jnp.exp(s - m_new), axis=1, keepdims=True)
        return m_new, l

    m, l = lax.fori_loop(
        0, count, stats, (jnp.full((stacked, 1), -1e30, jnp.float32), jnp.zeros((stacked, 1), jnp.float32))
    )
    lse = m + jnp.log(l)

    def forward(i, o):
        start = first_key(i)
        p = jnp.exp(tiles_ref[i] - lse)
        tiles_ref[i] = p
        return o + jnp.dot(
            p.astype(jnp.bfloat16), v_ref[pl.ds(start, SPAN_ROWS), :], preferred_element_type=jnp.float32
        )

    o = lax.fori_loop(0, count, forward, jnp.zeros((stacked, DH), jnp.float32))
    delta = jnp.sum(gr.astype(jnp.float32) * o.astype(jnp.bfloat16).astype(jnp.float32), axis=1, keepdims=True)

    def backward(i, dq):
        start = first_key(i)
        kb = k_ref[pl.ds(start, SPAN_ROWS), :]
        vb = v_ref[pl.ds(start, SPAN_ROWS), :]
        p = tiles_ref[i]
        dp = lax.dot_general(gr, vb, (((1,), (1,)), ((), ())), preferred_element_type=jnp.float32)
        ds = (p * (dp - delta)).astype(jnp.bfloat16)
        dk_ref[pl.ds(start, SPAN_ROWS), :] += lax.dot_general(
            ds, q, (((0,), (0,)), ((), ())), preferred_element_type=jnp.float32
        )
        dv_ref[pl.ds(start, SPAN_ROWS), :] += lax.dot_general(
            p.astype(jnp.bfloat16), gr, (((0,), (0,)), ((), ())), preferred_element_type=jnp.float32
        )
        return dq + jnp.dot(ds, kb, preferred_element_type=jnp.float32)

    dq = lax.fori_loop(0, count, backward, jnp.zeros((stacked, DH), jnp.float32)) * scale
    for g in range(heads):
        dq_ref[:, g * DH : (g + 1) * DH] = dq[g * rows : (g + 1) * rows]

    @pl.when(span == pl.num_programs(1) - 1)
    def _():
        dk_ref[...] = dk_ref[...] * scale


def attention(span_list, span_count, query, grad, keys, values, qpos, qdoc, kpos, kdoc, interpret=False):
    rows, width = query.shape
    keys_len, kv_width = keys.shape
    groups = width // kv_width
    heads = kv_width // DH
    q_spec = pl.BlockSpec((SPAN_ROWS, groups * DH), lambda c, s, *_: (s, c))
    k_spec = pl.BlockSpec((keys_len, DH), lambda c, s, *_: (0, c))
    col_spec = pl.BlockSpec((SPAN_ROWS, 1), lambda c, s, *_: (s, 0))
    row_spec = pl.BlockSpec((1, keys_len), lambda c, s, *_: (0, 0))
    return pl.pallas_call(
        attention_kernel,
        grid_spec=pltpu.PrefetchScalarGridSpec(
            num_scalar_prefetch=2,
            grid=(heads, rows // SPAN_ROWS),
            in_specs=[q_spec, q_spec, k_spec, k_spec, col_spec, col_spec, row_spec, row_spec],
            out_specs=[q_spec, k_spec, k_spec],
            scratch_shapes=[pltpu.VMEM((keys_len // SPAN_ROWS, groups * SPAN_ROWS, SPAN_ROWS), jnp.float32)],
        ),
        out_shape=[
            jax.ShapeDtypeStruct((rows, width), jnp.float32),
            jax.ShapeDtypeStruct((keys_len, kv_width), jnp.float32),
            jax.ShapeDtypeStruct((keys_len, kv_width), jnp.float32),
        ],
        compiler_params=pltpu.CompilerParams(dimension_semantics=("arbitrary", "arbitrary")),
        interpret=interpret,
    )(span_list, span_count, query, grad, keys, values, qpos, qdoc, kpos, kdoc)


def visible(query_pos, query_doc, key_pos, key_doc):
    return (key_pos[None, :] <= query_pos[:, None]) & (key_doc[None, :] == query_doc[:, None])


def local(query_in, key_in, value_in, grad_out, target, span_order, doc_ids):
    local_rows = query_in.shape[0]
    devices = lax.axis_size(("dp", "ctx"))
    ctx_size = lax.axis_size("ctx")
    packs = devices // ctx_size
    pack_len = local_rows * ctx_size
    capacity = (local_rows // devices + 2) * ctx_size
    q_cols = query_in.shape[1]
    k_cols = key_in.shape[1]
    q_width = q_cols // ctx_size
    k_width = k_cols // ctx_size
    ctx_ids = np.arange(ctx_size)
    kv_of = (ctx_ids // 4) * 2 + ctx_ids % 2
    half_of = (ctx_ids // 2) % 2
    block_of = 2 * kv_of + half_of
    ctx_of_block = np.argsort(block_of)

    pack_of = target // pack_len
    row_in_pack = target % pack_len
    onehot = (pack_of[:, None] == jnp.arange(packs, dtype=jnp.int32)[None, :]).astype(jnp.int32)
    slot = jnp.sum((jnp.cumsum(onehot, axis=0) - onehot) * onehot, axis=1)
    dest_pack = pack_of[:, None]
    dest_ctx = jnp.asarray(ctx_ids, jnp.int32)[None, :]
    dest_slot = slot[:, None]

    payload = jnp.concatenate(
        [
            query_in.reshape(local_rows, ctx_size, q_width)[:, block_of],
            grad_out.reshape(local_rows, ctx_size, q_width)[:, block_of],
            key_in.reshape(local_rows, k_cols // DH, DH)[:, kv_of],
            value_in.reshape(local_rows, k_cols // DH, DH)[:, kv_of],
        ],
        axis=2,
    )
    width = payload.shape[2]
    flat_slot = pack_of * capacity + slot
    picks = jnp.arange(packs * capacity, dtype=jnp.int32)[:, None] == flat_slot[None, :]
    holder = (
        jnp.dot(
            picks.astype(jnp.bfloat16),
            payload.reshape(local_rows, ctx_size * width),
            preferred_element_type=jnp.float32,
        )
        .astype(jnp.bfloat16)
        .reshape(packs, capacity, ctx_size, width)
        .transpose(0, 2, 1, 3)
        .reshape(devices * capacity, width)
    )
    places = jnp.broadcast_to(
        jnp.sum(jnp.where(picks, (row_in_pack + 1)[None, :], 0), axis=1).reshape(packs, 1, capacity),
        (packs, ctx_size, capacity),
    ).reshape(devices * capacity)
    got = lax.all_to_all(holder, ("dp", "ctx"), split_axis=0, concat_axis=0, tiled=True)
    got_places = lax.all_to_all(places, ("dp", "ctx"), split_axis=0, concat_axis=0, tiled=True)
    span_seq = span_order[0]
    span_rows = pack_len // span_seq.shape[0]
    packed_row = got_places - 1
    span_pos = jnp.sum(
        jnp.where(
            (packed_row // span_rows)[:, None] == jnp.arange(span_seq.shape[0], dtype=jnp.int32)[None, :],
            span_seq[None, :],
            0,
        ),
        axis=1,
    )
    landing = jnp.where(packed_row >= 0, span_pos * span_rows + packed_row % span_rows, pack_len)
    rows = jnp.zeros((pack_len, width), jnp.bfloat16).at[landing].set(got, mode="drop")
    query = rows[:, :q_width]
    grad_rows = rows[:, q_width : 2 * q_width]
    keys = rows[:, 2 * q_width : 2 * q_width + DH]
    values = rows[:, 2 * q_width + DH : 2 * q_width + 2 * DH]

    doc_block = jnp.broadcast_to(doc_ids[0].astype(jnp.bfloat16)[:, None], (local_rows, 128))
    doc_all = lax.all_gather(doc_block, "ctx", axis=0, tiled=True)[:, 0].astype(jnp.int32)
    positions = jnp.arange(pack_len, dtype=jnp.int32)

    spans = pack_len // SPAN_ROWS
    tile_docs = doc_all.reshape(spans, SPAN_ROWS)
    first_doc = tile_docs[:, 0]
    last_doc = tile_docs[:, -1]
    tile_ids = jnp.arange(spans)
    active = (
        (tile_ids[None, :] <= tile_ids[:, None])
        & (first_doc[None, :] <= last_doc[:, None])
        & (first_doc[:, None] <= last_doc[None, :])
    )
    span_count = jnp.sum(active.astype(jnp.int32), axis=1)
    rank = jnp.cumsum(active.astype(jnp.int32), axis=1) - 1
    slot_of = jnp.where(active, rank + spans * jnp.arange(spans)[:, None], spans * spans)
    span_list = (
        jnp.zeros((spans * spans,), jnp.int32)
        .at[slot_of.reshape(-1)]
        .set(jnp.tile(jnp.arange(spans, dtype=jnp.int32), spans), mode="drop")
    )
    dquery, dkey, dvalue = attention(
        span_list,
        span_count,
        query,
        grad_rows,
        keys,
        values,
        positions.reshape(pack_len, 1),
        doc_all.reshape(pack_len, 1),
        positions.reshape(1, pack_len),
        doc_all.reshape(1, pack_len),
    )

    half = jnp.asarray(half_of, jnp.int32)[lax.axis_index("ctx")]
    split_key = dkey.reshape(pack_len, 2, k_width)
    split_value = dvalue.reshape(pack_len, 2, k_width)
    mine = jnp.concatenate(
        [lax.dynamic_index_in_dim(split_key, half, 1, False), lax.dynamic_index_in_dim(split_value, half, 1, False)],
        axis=1,
    )
    other = jnp.concatenate(
        [
            lax.dynamic_index_in_dim(split_key, 1 - half, 1, False),
            lax.dynamic_index_in_dim(split_value, 1 - half, 1, False),
        ],
        axis=1,
    ).astype(jnp.bfloat16)
    partner = [(int(c), int(c) ^ 2) for c in ctx_ids]
    key_value = mine + lax.ppermute(other, "ctx", partner).astype(jnp.float32)

    result = jnp.concatenate([dquery.astype(jnp.bfloat16), key_value.astype(jnp.bfloat16)], axis=1)
    source_rows = jnp.where(landing < pack_len, landing, 0)
    back = (
        lax.all_to_all(result[source_rows], ("dp", "ctx"), split_axis=0, concat_axis=0, tiled=True)
        .reshape(packs, ctx_size, capacity, result.shape[1])
        .transpose(0, 2, 1, 3)
        .reshape(packs * capacity, ctx_size, result.shape[1])
    )
    pieces = back[flat_slot][:, ctx_of_block].astype(jnp.float32)
    return (
        pieces[:, :, :q_width].reshape(local_rows, q_cols),
        pieces[:, :, q_width : q_width + k_width].reshape(local_rows, k_cols),
        pieces[:, :, q_width + k_width :].reshape(local_rows, k_cols),
    )


def solution(mesh):
    placed = (
        P(("dp", "ctx"), None),
        P(("dp", "ctx"), None),
        P(("dp", "ctx"), None),
        P(("dp", "ctx"), None),
        P(("dp", "ctx")),
        P("dp", None),
        P("dp", "ctx"),
    )
    return jax.shard_map(
        local,
        mesh=mesh,
        in_specs=placed,
        out_specs=(P(("dp", "ctx"), None), P(("dp", "ctx"), None), P(("dp", "ctx"), None)),
        check_vma=False,
    )
```

```python
import jax
import numpy as np
import jax.numpy as jnp
from jax import lax
from jax.sharding import PartitionSpec as P
from jax.experimental import pallas as pl
from jax.experimental.pallas import tpu as pltpu

HQ = 16
HK = 4
DH = 128


SPAN_ROWS = 256


def attention_kernel(
    list_ref, count_ref, q_ref, g_ref, k_ref, v_ref, qpos_ref, qdoc_ref, kpos_ref, kdoc_ref,
    dq_ref, dk_ref, dv_ref, tiles_ref,
):
    scale = DH ** (-0.5)
    rows = q_ref.shape[0]
    heads = q_ref.shape[1] // DH
    stacked = heads * rows
    span = pl.program_id(1)
    spans = list_ref.shape[0] // pl.num_programs(1)
    count = count_ref[span]

    @pl.when(span == 0)
    def _():
        dk_ref[...] = jnp.zeros(dk_ref.shape, jnp.float32)
        dv_ref[...] = jnp.zeros(dv_ref.shape, jnp.float32)

    qpos = qpos_ref[...]
    qdoc = qdoc_ref[...]
    q = jnp.concatenate([q_ref[:, g * DH : (g + 1) * DH] for g in range(heads)], axis=0)
    gr = jnp.concatenate([g_ref[:, g * DH : (g + 1) * DH] for g in range(heads)], axis=0)

    def first_key(i):
        return pl.multiple_of(list_ref[span * spans + i] * SPAN_ROWS, SPAN_ROWS)

    def stats(i, carry):
        m, l = carry
        start = first_key(i)
        kp = kpos_ref[:, pl.ds(start, SPAN_ROWS)]
        kd = kdoc_ref[:, pl.ds(start, SPAN_ROWS)]
        allowed = (kp <= qpos) & (kd == qdoc)
        s = lax.dot_general(
            q, k_ref[pl.ds(start, SPAN_ROWS), :], (((1,), (1,)), ((), ())),
            preferred_element_type=jnp.float32,
        ) * scale
        s = jnp.where(allowed[None], s.reshape(heads, rows, SPAN_ROWS), -jnp.inf).reshape(stacked, SPAN_ROWS)
        tiles_ref[i] = s
        m_new = jnp.maximum(m, jnp.max(s, axis=1, keepdims=True))
        l = l * jnp.exp(m - m_new) + jnp.sum(jnp.exp(s - m_new), axis=1, keepdims=True)
        return m_new, l

    m, l = lax.fori_loop(
        0, count, stats, (jnp.full((stacked, 1), -1e30, jnp.float32), jnp.zeros((stacked, 1), jnp.float32))
    )
    lse = m + jnp.log(l)

    def forward(i, o):
        start = first_key(i)
        p = jnp.exp(tiles_ref[i] - lse)
        tiles_ref[i] = p
        return o + jnp.dot(
            p.astype(jnp.bfloat16), v_ref[pl.ds(start, SPAN_ROWS), :], preferred_element_type=jnp.float32
        )

    o = lax.fori_loop(0, count, forward, jnp.zeros((stacked, DH), jnp.float32))
    delta = jnp.sum(gr.astype(jnp.float32) * o.astype(jnp.bfloat16).astype(jnp.float32), axis=1, keepdims=True)

    def backward(i, dq):
        start = first_key(i)
        kb = k_ref[pl.ds(start, SPAN_ROWS), :]
        vb = v_ref[pl.ds(start, SPAN_ROWS), :]
        p = tiles_ref[i]
        dp = lax.dot_general(gr, vb, (((1,), (1,)), ((), ())), preferred_element_type=jnp.float32)
        ds = (p * (dp - delta)).astype(jnp.bfloat16)
        dk_ref[pl.ds(start, SPAN_ROWS), :] += lax.dot_general(
            ds, q, (((0,), (0,)), ((), ())), preferred_element_type=jnp.float32
        )
        dv_ref[pl.ds(start, SPAN_ROWS), :] += lax.dot_general(
            p.astype(jnp.bfloat16), gr, (((0,), (0,)), ((), ())), preferred_element_type=jnp.float32
        )
        return dq + jnp.dot(ds, kb, preferred_element_type=jnp.float32)

    dq = lax.fori_loop(0, count, backward, jnp.zeros((stacked, DH), jnp.float32)) * scale
    for g in range(heads):
        dq_ref[:, g * DH : (g + 1) * DH] = dq[g * rows : (g + 1) * rows]

    @pl.when(span == pl.num_programs(1) - 1)
    def _():
        dk_ref[...] = dk_ref[...] * scale


def attention(span_list, span_count, query, grad, keys, values, qpos, qdoc, kpos, kdoc, interpret=False):
    rows, width = query.shape
    keys_len, kv_width = keys.shape
    groups = width // kv_width
    heads = kv_width // DH
    q_spec = pl.BlockSpec((SPAN_ROWS, groups * DH), lambda c, s, *_: (s, c))
    k_spec = pl.BlockSpec((keys_len, DH), lambda c, s, *_: (0, c))
    col_spec = pl.BlockSpec((SPAN_ROWS, 1), lambda c, s, *_: (s, 0))
    row_spec = pl.BlockSpec((1, keys_len), lambda c, s, *_: (0, 0))
    return pl.pallas_call(
        attention_kernel,
        grid_spec=pltpu.PrefetchScalarGridSpec(
            num_scalar_prefetch=2,
            grid=(heads, rows // SPAN_ROWS),
            in_specs=[q_spec, q_spec, k_spec, k_spec, col_spec, col_spec, row_spec, row_spec],
            out_specs=[q_spec, k_spec, k_spec],
            scratch_shapes=[pltpu.VMEM((keys_len // SPAN_ROWS, groups * SPAN_ROWS, SPAN_ROWS), jnp.float32)],
        ),
        out_shape=[
            jax.ShapeDtypeStruct((rows, width), jnp.float32),
            jax.ShapeDtypeStruct((keys_len, kv_width), jnp.float32),
            jax.ShapeDtypeStruct((keys_len, kv_width), jnp.float32),
        ],
        compiler_params=pltpu.CompilerParams(dimension_semantics=("arbitrary", "arbitrary")),
        interpret=interpret,
    )(span_list, span_count, query, grad, keys, values, qpos, qdoc, kpos, kdoc)


def visible(query_pos, query_doc, key_pos, key_doc):
    return (key_pos[None, :] <= query_pos[:, None]) & (key_doc[None, :] == query_doc[:, None])


def local(query_in, key_in, value_in, grad_out, target, span_order, doc_ids):
    local_rows = query_in.shape[0]
    devices = lax.axis_size(("dp", "ctx"))
    ctx_size = lax.axis_size("ctx")
    packs = devices // ctx_size
    pack_len = local_rows * ctx_size
    capacity = (local_rows // devices + 2) * ctx_size
    q_cols = query_in.shape[1]
    k_cols = key_in.shape[1]
    q_width = q_cols // ctx_size
    k_width = k_cols // ctx_size
    ctx_ids = np.arange(ctx_size)
    kv_of = (ctx_ids // 4) * 2 + ctx_ids % 2
    half_of = (ctx_ids // 2) % 2
    block_of = 2 * kv_of + half_of
    ctx_of_block = np.argsort(block_of)

    pack_of = target // pack_len
    row_in_pack = target % pack_len
    onehot = (pack_of[:, None] == jnp.arange(packs, dtype=jnp.int32)[None, :]).astype(jnp.int32)
    slot = jnp.sum((jnp.cumsum(onehot, axis=0) - onehot) * onehot, axis=1)
    dest_pack = pack_of[:, None]
    dest_ctx = jnp.asarray(ctx_ids, jnp.int32)[None, :]
    dest_slot = slot[:, None]

    payload = jnp.concatenate(
        [
            query_in.reshape(local_rows, ctx_size, q_width)[:, block_of],
            grad_out.reshape(local_rows, ctx_size, q_width)[:, block_of],
            key_in.reshape(local_rows, k_cols // DH, DH)[:, kv_of],
            value_in.reshape(local_rows, k_cols // DH, DH)[:, kv_of],
        ],
        axis=2,
    )
    width = payload.shape[2]
    flat_slot = pack_of * capacity + slot
    picks = jnp.arange(packs * capacity, dtype=jnp.int32)[:, None] == flat_slot[None, :]
    holder = (
        jnp.dot(
            picks.astype(jnp.bfloat16),
            payload.reshape(local_rows, ctx_size * width),
            preferred_element_type=jnp.float32,
        )
        .astype(jnp.bfloat16)
        .reshape(packs, capacity, ctx_size, width)
        .transpose(0, 2, 1, 3)
        .reshape(devices * capacity, width)
    )
    places = jnp.broadcast_to(
        jnp.sum(jnp.where(picks, (row_in_pack + 1)[None, :], 0), axis=1).reshape(packs, 1, capacity),
        (packs, ctx_size, capacity),
    ).reshape(devices * capacity)
    got = lax.all_to_all(holder, ("dp", "ctx"), split_axis=0, concat_axis=0, tiled=True)
    got_places = lax.all_to_all(places, ("dp", "ctx"), split_axis=0, concat_axis=0, tiled=True)
    span_seq = span_order[0]
    span_rows = pack_len // span_seq.shape[0]
    packed_row = got_places - 1
    span_pos = jnp.sum(
        jnp.where(
            (packed_row // span_rows)[:, None] == jnp.arange(span_seq.shape[0], dtype=jnp.int32)[None, :],
            span_seq[None, :],
            0,
        ),
        axis=1,
    )
    landing = jnp.where(packed_row >= 0, span_pos * span_rows + packed_row % span_rows, pack_len)
    lands = jnp.arange(pack_len, dtype=jnp.int32)[:, None] == landing[None, :]
    rows = jnp.dot(lands.astype(jnp.bfloat16), got, preferred_element_type=jnp.float32).astype(jnp.bfloat16)
    query = rows[:, :q_width]
    grad_rows = rows[:, q_width : 2 * q_width]
    keys = rows[:, 2 * q_width : 2 * q_width + DH]
    values = rows[:, 2 * q_width + DH : 2 * q_width + 2 * DH]

    doc_block = jnp.broadcast_to(doc_ids[0].astype(jnp.bfloat16)[:, None], (local_rows, 128))
    doc_all = lax.all_gather(doc_block, "ctx", axis=0, tiled=True)[:, 0].astype(jnp.int32)
    positions = jnp.arange(pack_len, dtype=jnp.int32)

    spans = pack_len // SPAN_ROWS
    tile_docs = doc_all.reshape(spans, SPAN_ROWS)
    first_doc = tile_docs[:, 0]
    last_doc = tile_docs[:, -1]
    tile_ids = jnp.arange(spans)
    active = (
        (tile_ids[None, :] <= tile_ids[:, None])
        & (first_doc[None, :] <= last_doc[:, None])
        & (first_doc[:, None] <= last_doc[None, :])
    )
    span_count = jnp.sum(active.astype(jnp.int32), axis=1)
    rank = jnp.cumsum(active.astype(jnp.int32), axis=1) - 1
    slot_of = jnp.where(active, rank + spans * jnp.arange(spans)[:, None], spans * spans)
    span_list = (
        jnp.zeros((spans * spans,), jnp.int32)
        .at[slot_of.reshape(-1)]
        .set(jnp.tile(jnp.arange(spans, dtype=jnp.int32), spans), mode="drop")
    )
    dquery, dkey, dvalue = attention(
        span_list,
        span_count,
        query,
        grad_rows,
        keys,
        values,
        positions.reshape(pack_len, 1),
        doc_all.reshape(pack_len, 1),
        positions.reshape(1, pack_len),
        doc_all.reshape(1, pack_len),
    )

    half = jnp.asarray(half_of, jnp.int32)[lax.axis_index("ctx")]
    split_key = dkey.reshape(pack_len, 2, k_width)
    split_value = dvalue.reshape(pack_len, 2, k_width)
    mine = jnp.concatenate(
        [lax.dynamic_index_in_dim(split_key, half, 1, False), lax.dynamic_index_in_dim(split_value, half, 1, False)],
        axis=1,
    )
    other = jnp.concatenate(
        [
            lax.dynamic_index_in_dim(split_key, 1 - half, 1, False),
            lax.dynamic_index_in_dim(split_value, 1 - half, 1, False),
        ],
        axis=1,
    ).astype(jnp.bfloat16)
    partner = [(int(c), int(c) ^ 2) for c in ctx_ids]
    key_value = mine + lax.ppermute(other, "ctx", partner).astype(jnp.float32)

    result = jnp.concatenate([dquery.astype(jnp.bfloat16), key_value.astype(jnp.bfloat16)], axis=1)
    back = (
        lax.all_to_all(
            lax.dot_general(
                lands.astype(jnp.bfloat16), result, (((0,), (0,)), ((), ())), preferred_element_type=jnp.float32
            ).astype(jnp.bfloat16),
            ("dp", "ctx"),
            split_axis=0,
            concat_axis=0,
            tiled=True,
        )
        .reshape(packs, ctx_size, capacity, result.shape[1])
        .transpose(0, 2, 1, 3)
        .reshape(packs * capacity, ctx_size, result.shape[1])
    )
    pieces = back[flat_slot][:, ctx_of_block].astype(jnp.float32)
    return (
        pieces[:, :, :q_width].reshape(local_rows, q_cols),
        pieces[:, :, q_width : q_width + k_width].reshape(local_rows, k_cols),
        pieces[:, :, q_width + k_width :].reshape(local_rows, k_cols),
    )


def solution(mesh):
    placed = (
        P(("dp", "ctx"), None),
        P(("dp", "ctx"), None),
        P(("dp", "ctx"), None),
        P(("dp", "ctx"), None),
        P(("dp", "ctx")),
        P("dp", None),
        P("dp", "ctx"),
    )
    return jax.shard_map(
        local,
        mesh=mesh,
        in_specs=placed,
        out_specs=(P(("dp", "ctx"), None), P(("dp", "ctx"), None), P(("dp", "ctx"), None)),
        check_vma=False,
    )
```

```python
import jax
import numpy as np
import jax.numpy as jnp
from jax import lax
from jax.sharding import PartitionSpec as P
from jax.experimental import pallas as pl
from jax.experimental.pallas import tpu as pltpu

HQ = 16
HK = 4
DH = 128


SPAN_ROWS = 256
QUERY_ROWS = 512


def attention_kernel(
    list_ref, count_ref, q_ref, g_ref, k_ref, v_ref, qpos_ref, qdoc_ref, kpos_ref, kdoc_ref,
    dq_ref, dk_ref, dv_ref, tiles_ref,
):
    scale = DH ** (-0.5)
    rows = q_ref.shape[0]
    heads = q_ref.shape[1] // DH
    stacked = heads * rows
    span = pl.program_id(1)
    spans = list_ref.shape[0] // pl.num_programs(1)
    count = count_ref[span]

    @pl.when(span == 0)
    def _():
        dk_ref[...] = jnp.zeros(dk_ref.shape, jnp.float32)
        dv_ref[...] = jnp.zeros(dv_ref.shape, jnp.float32)

    qpos = qpos_ref[...]
    qdoc = qdoc_ref[...]
    q = jnp.concatenate([q_ref[:, g * DH : (g + 1) * DH] for g in range(heads)], axis=0)
    gr = jnp.concatenate([g_ref[:, g * DH : (g + 1) * DH] for g in range(heads)], axis=0)

    def first_key(i):
        return pl.multiple_of(list_ref[span * spans + i] * SPAN_ROWS, SPAN_ROWS)

    def stats(i, carry):
        m, l = carry
        start = first_key(i)
        kp = kpos_ref[:, pl.ds(start, SPAN_ROWS)]
        kd = kdoc_ref[:, pl.ds(start, SPAN_ROWS)]
        allowed = (kp <= qpos) & (kd == qdoc)
        s = lax.dot_general(
            q, k_ref[pl.ds(start, SPAN_ROWS), :], (((1,), (1,)), ((), ())),
            preferred_element_type=jnp.float32,
        ) * scale
        s = jnp.where(allowed[None], s.reshape(heads, rows, SPAN_ROWS), -jnp.inf).reshape(stacked, SPAN_ROWS)
        tiles_ref[i] = s
        m_new = jnp.maximum(m, jnp.max(s, axis=1, keepdims=True))
        l = l * jnp.exp(m - m_new) + jnp.sum(jnp.exp(s - m_new), axis=1, keepdims=True)
        return m_new, l

    m, l = lax.fori_loop(
        0, count, stats, (jnp.full((stacked, 1), -1e30, jnp.float32), jnp.zeros((stacked, 1), jnp.float32))
    )
    lse = m + jnp.log(l)

    def forward(i, o):
        start = first_key(i)
        p = jnp.exp(tiles_ref[i] - lse)
        tiles_ref[i] = p
        return o + jnp.dot(
            p.astype(jnp.bfloat16), v_ref[pl.ds(start, SPAN_ROWS), :], preferred_element_type=jnp.float32
        )

    o = lax.fori_loop(0, count, forward, jnp.zeros((stacked, DH), jnp.float32))
    delta = jnp.sum(gr.astype(jnp.float32) * o.astype(jnp.bfloat16).astype(jnp.float32), axis=1, keepdims=True)

    def backward(i, dq):
        start = first_key(i)
        kb = k_ref[pl.ds(start, SPAN_ROWS), :]
        vb = v_ref[pl.ds(start, SPAN_ROWS), :]
        p = tiles_ref[i]
        dp = lax.dot_general(gr, vb, (((1,), (1,)), ((), ())), preferred_element_type=jnp.float32)
        ds = (p * (dp - delta)).astype(jnp.bfloat16)
        dk_ref[pl.ds(start, SPAN_ROWS), :] += lax.dot_general(
            ds, q, (((0,), (0,)), ((), ())), preferred_element_type=jnp.float32
        )
        dv_ref[pl.ds(start, SPAN_ROWS), :] += lax.dot_general(
            p.astype(jnp.bfloat16), gr, (((0,), (0,)), ((), ())), preferred_element_type=jnp.float32
        )
        return dq + jnp.dot(ds, kb, preferred_element_type=jnp.float32)

    dq = lax.fori_loop(0, count, backward, jnp.zeros((stacked, DH), jnp.float32)) * scale
    for g in range(heads):
        dq_ref[:, g * DH : (g + 1) * DH] = dq[g * rows : (g + 1) * rows]

    @pl.when(span == pl.num_programs(1) - 1)
    def _():
        dk_ref[...] = dk_ref[...] * scale


def attention(span_list, span_count, query, grad, keys, values, qpos, qdoc, kpos, kdoc, interpret=False):
    rows, width = query.shape
    keys_len, kv_width = keys.shape
    groups = width // kv_width
    heads = kv_width // DH
    q_spec = pl.BlockSpec((QUERY_ROWS, groups * DH), lambda c, s, *_: (s, c))
    k_spec = pl.BlockSpec((keys_len, DH), lambda c, s, *_: (0, c))
    col_spec = pl.BlockSpec((QUERY_ROWS, 1), lambda c, s, *_: (s, 0))
    row_spec = pl.BlockSpec((1, keys_len), lambda c, s, *_: (0, 0))
    return pl.pallas_call(
        attention_kernel,
        grid_spec=pltpu.PrefetchScalarGridSpec(
            num_scalar_prefetch=2,
            grid=(heads, rows // QUERY_ROWS),
            in_specs=[q_spec, q_spec, k_spec, k_spec, col_spec, col_spec, row_spec, row_spec],
            out_specs=[q_spec, k_spec, k_spec],
            scratch_shapes=[pltpu.VMEM((keys_len // SPAN_ROWS, groups * QUERY_ROWS, SPAN_ROWS), jnp.float32)],
        ),
        out_shape=[
            jax.ShapeDtypeStruct((rows, width), jnp.float32),
            jax.ShapeDtypeStruct((keys_len, kv_width), jnp.float32),
            jax.ShapeDtypeStruct((keys_len, kv_width), jnp.float32),
        ],
        compiler_params=pltpu.CompilerParams(
            dimension_semantics=("arbitrary", "arbitrary"), vmem_limit_bytes=48 * 1024 * 1024
        ),
        interpret=interpret,
    )(span_list, span_count, query, grad, keys, values, qpos, qdoc, kpos, kdoc)


def visible(query_pos, query_doc, key_pos, key_doc):
    return (key_pos[None, :] <= query_pos[:, None]) & (key_doc[None, :] == query_doc[:, None])


def local(query_in, key_in, value_in, grad_out, target, span_order, doc_ids):
    local_rows = query_in.shape[0]
    devices = lax.axis_size(("dp", "ctx"))
    ctx_size = lax.axis_size("ctx")
    packs = devices // ctx_size
    pack_len = local_rows * ctx_size
    capacity = (local_rows // devices + 2) * ctx_size
    q_cols = query_in.shape[1]
    k_cols = key_in.shape[1]
    q_width = q_cols // ctx_size
    k_width = k_cols // ctx_size
    ctx_ids = np.arange(ctx_size)
    kv_of = (ctx_ids // 4) * 2 + ctx_ids % 2
    half_of = (ctx_ids // 2) % 2
    block_of = 2 * kv_of + half_of
    ctx_of_block = np.argsort(block_of)

    pack_of = target // pack_len
    row_in_pack = target % pack_len
    onehot = (pack_of[:, None] == jnp.arange(packs, dtype=jnp.int32)[None, :]).astype(jnp.int32)
    slot = jnp.sum((jnp.cumsum(onehot, axis=0) - onehot) * onehot, axis=1)
    dest_pack = pack_of[:, None]
    dest_ctx = jnp.asarray(ctx_ids, jnp.int32)[None, :]
    dest_slot = slot[:, None]

    payload = jnp.concatenate(
        [
            query_in.reshape(local_rows, ctx_size, q_width)[:, block_of],
            grad_out.reshape(local_rows, ctx_size, q_width)[:, block_of],
            key_in.reshape(local_rows, k_cols // DH, DH)[:, kv_of],
            value_in.reshape(local_rows, k_cols // DH, DH)[:, kv_of],
        ],
        axis=2,
    )
    width = payload.shape[2]
    flat_slot = pack_of * capacity + slot
    picks = jnp.arange(packs * capacity, dtype=jnp.int32)[:, None] == flat_slot[None, :]
    holder = (
        jnp.dot(
            picks.astype(jnp.bfloat16),
            payload.reshape(local_rows, ctx_size * width),
            preferred_element_type=jnp.float32,
        )
        .astype(jnp.bfloat16)
        .reshape(packs, capacity, ctx_size, width)
        .transpose(0, 2, 1, 3)
        .reshape(devices * capacity, width)
    )
    places = jnp.broadcast_to(
        jnp.sum(jnp.where(picks, (row_in_pack + 1)[None, :], 0), axis=1).reshape(packs, 1, capacity),
        (packs, ctx_size, capacity),
    ).reshape(devices * capacity)
    got = lax.all_to_all(holder, ("dp", "ctx"), split_axis=0, concat_axis=0, tiled=True)
    got_places = lax.all_to_all(places, ("dp", "ctx"), split_axis=0, concat_axis=0, tiled=True)
    span_seq = span_order[0]
    span_rows = pack_len // span_seq.shape[0]
    packed_row = got_places - 1
    span_pos = jnp.sum(
        jnp.where(
            (packed_row // span_rows)[:, None] == jnp.arange(span_seq.shape[0], dtype=jnp.int32)[None, :],
            span_seq[None, :],
            0,
        ),
        axis=1,
    )
    landing = jnp.where(packed_row >= 0, span_pos * span_rows + packed_row % span_rows, pack_len)
    lands = jnp.arange(pack_len, dtype=jnp.int32)[:, None] == landing[None, :]
    rows = jnp.dot(lands.astype(jnp.bfloat16), got, preferred_element_type=jnp.float32).astype(jnp.bfloat16)
    query = rows[:, :q_width]
    grad_rows = rows[:, q_width : 2 * q_width]
    keys = rows[:, 2 * q_width : 2 * q_width + DH]
    values = rows[:, 2 * q_width + DH : 2 * q_width + 2 * DH]

    doc_block = jnp.broadcast_to(doc_ids[0].astype(jnp.bfloat16)[:, None], (local_rows, 128))
    doc_all = lax.all_gather(doc_block, "ctx", axis=0, tiled=True)[:, 0].astype(jnp.int32)
    positions = jnp.arange(pack_len, dtype=jnp.int32)

    spans = pack_len // SPAN_ROWS
    query_tiles = pack_len // QUERY_ROWS
    tile_docs = doc_all.reshape(spans, SPAN_ROWS)
    query_docs = doc_all.reshape(query_tiles, QUERY_ROWS)
    tile_ids = jnp.arange(spans)
    query_ids = jnp.arange(query_tiles)
    active = (
        (tile_ids[None, :] * SPAN_ROWS < (query_ids[:, None] + 1) * QUERY_ROWS)
        & (tile_docs[None, :, 0] <= query_docs[:, None, -1])
        & (query_docs[:, None, 0] <= tile_docs[None, :, -1])
    )
    span_count = jnp.sum(active.astype(jnp.int32), axis=1)
    rank = jnp.cumsum(active.astype(jnp.int32), axis=1) - 1
    slot_of = jnp.where(active, rank + spans * query_ids[:, None], spans * query_tiles)
    span_list = (
        jnp.zeros((spans * query_tiles,), jnp.int32)
        .at[slot_of.reshape(-1)]
        .set(jnp.tile(jnp.arange(spans, dtype=jnp.int32), query_tiles), mode="drop")
    )
    dquery, dkey, dvalue = attention(
        span_list,
        span_count,
        query,
        grad_rows,
        keys,
        values,
        positions.reshape(pack_len, 1),
        doc_all.reshape(pack_len, 1),
        positions.reshape(1, pack_len),
        doc_all.reshape(1, pack_len),
    )

    half = jnp.asarray(half_of, jnp.int32)[lax.axis_index("ctx")]
    split_key = dkey.reshape(pack_len, 2, k_width)
    split_value = dvalue.reshape(pack_len, 2, k_width)
    mine = jnp.concatenate(
        [lax.dynamic_index_in_dim(split_key, half, 1, False), lax.dynamic_index_in_dim(split_value, half, 1, False)],
        axis=1,
    )
    other = jnp.concatenate(
        [
            lax.dynamic_index_in_dim(split_key, 1 - half, 1, False),
            lax.dynamic_index_in_dim(split_value, 1 - half, 1, False),
        ],
        axis=1,
    ).astype(jnp.bfloat16)
    partner = [(int(c), int(c) ^ 2) for c in ctx_ids]
    key_value = mine + lax.ppermute(other, "ctx", partner).astype(jnp.float32)

    result = jnp.concatenate([dquery.astype(jnp.bfloat16), key_value.astype(jnp.bfloat16)], axis=1)
    back = (
        lax.all_to_all(
            lax.dot_general(
                lands.astype(jnp.bfloat16), result, (((0,), (0,)), ((), ())), preferred_element_type=jnp.float32
            ).astype(jnp.bfloat16),
            ("dp", "ctx"),
            split_axis=0,
            concat_axis=0,
            tiled=True,
        )
        .reshape(packs, ctx_size, capacity, result.shape[1])
        .transpose(0, 2, 1, 3)
        .reshape(packs * capacity, ctx_size, result.shape[1])
    )
    pieces = back[flat_slot][:, ctx_of_block].astype(jnp.float32)
    return (
        pieces[:, :, :q_width].reshape(local_rows, q_cols),
        pieces[:, :, q_width : q_width + k_width].reshape(local_rows, k_cols),
        pieces[:, :, q_width + k_width :].reshape(local_rows, k_cols),
    )


def solution(mesh):
    placed = (
        P(("dp", "ctx"), None),
        P(("dp", "ctx"), None),
        P(("dp", "ctx"), None),
        P(("dp", "ctx"), None),
        P(("dp", "ctx")),
        P("dp", None),
        P("dp", "ctx"),
    )
    return jax.shard_map(
        local,
        mesh=mesh,
        in_specs=placed,
        out_specs=(P(("dp", "ctx"), None), P(("dp", "ctx"), None), P(("dp", "ctx"), None)),
        check_vma=False,
    )
```

```python
import jax
import numpy as np
import jax.numpy as jnp
from jax import lax
from jax.sharding import PartitionSpec as P
from jax.experimental import pallas as pl
from jax.experimental.pallas import tpu as pltpu

HQ = 16
HK = 4
DH = 128


SPAN_ROWS = 256
QUERY_ROWS = 512


def attention_kernel(
    list_ref, count_ref, q_ref, g_ref, k_ref, v_ref, qpos_ref, qdoc_ref, kpos_ref, kdoc_ref,
    dq_ref, dk_ref, dv_ref, tiles_ref,
):
    scale = DH ** (-0.5)
    rows = q_ref.shape[0]
    heads = q_ref.shape[1] // DH
    stacked = heads * rows
    span = pl.program_id(1)
    spans = list_ref.shape[0] // pl.num_programs(1)
    count = count_ref[span]

    @pl.when(span == 0)
    def _():
        dk_ref[...] = jnp.zeros(dk_ref.shape, jnp.float32)
        dv_ref[...] = jnp.zeros(dv_ref.shape, jnp.float32)

    qpos = qpos_ref[...]
    qdoc = qdoc_ref[...]
    q = jnp.concatenate([q_ref[:, g * DH : (g + 1) * DH] for g in range(heads)], axis=0)
    gr = jnp.concatenate([g_ref[:, g * DH : (g + 1) * DH] for g in range(heads)], axis=0)

    def first_key(i):
        return pl.multiple_of(list_ref[span * spans + i] * SPAN_ROWS, SPAN_ROWS)

    def stats(i, carry):
        m, l = carry
        start = first_key(i)
        kp = kpos_ref[:, pl.ds(start, SPAN_ROWS)]
        kd = kdoc_ref[:, pl.ds(start, SPAN_ROWS)]
        allowed = (kp <= qpos) & (kd == qdoc)
        s = lax.dot_general(
            q, k_ref[pl.ds(start, SPAN_ROWS), :], (((1,), (1,)), ((), ())),
            preferred_element_type=jnp.float32,
        ) * scale
        s = jnp.where(allowed[None], s.reshape(heads, rows, SPAN_ROWS), -jnp.inf).reshape(stacked, SPAN_ROWS)
        tiles_ref[i] = s
        m_new = jnp.maximum(m, jnp.max(s, axis=1, keepdims=True))
        l = l * jnp.exp(m - m_new) + jnp.sum(jnp.exp(s - m_new), axis=1, keepdims=True)
        return m_new, l

    m, l = lax.fori_loop(
        0, count, stats, (jnp.full((stacked, 1), -1e30, jnp.float32), jnp.zeros((stacked, 1), jnp.float32))
    )
    lse = m + jnp.log(l)

    def forward(i, o):
        start = first_key(i)
        p = jnp.exp(tiles_ref[i] - lse)
        tiles_ref[i] = p
        return o + jnp.dot(
            p.astype(jnp.bfloat16), v_ref[pl.ds(start, SPAN_ROWS), :], preferred_element_type=jnp.float32
        )

    o = lax.fori_loop(0, count, forward, jnp.zeros((stacked, DH), jnp.float32))
    delta = jnp.sum(gr.astype(jnp.float32) * o.astype(jnp.bfloat16).astype(jnp.float32), axis=1, keepdims=True)

    def backward(i, dq):
        start = first_key(i)
        kb = k_ref[pl.ds(start, SPAN_ROWS), :]
        vb = v_ref[pl.ds(start, SPAN_ROWS), :]
        p = tiles_ref[i]
        dp = lax.dot_general(gr, vb, (((1,), (1,)), ((), ())), preferred_element_type=jnp.float32)
        ds = (p * (dp - delta)).astype(jnp.bfloat16)
        dk_ref[pl.ds(start, SPAN_ROWS), :] += lax.dot_general(
            ds, q, (((0,), (0,)), ((), ())), preferred_element_type=jnp.float32
        )
        dv_ref[pl.ds(start, SPAN_ROWS), :] += lax.dot_general(
            p.astype(jnp.bfloat16), gr, (((0,), (0,)), ((), ())), preferred_element_type=jnp.float32
        )
        return dq + jnp.dot(ds, kb, preferred_element_type=jnp.float32)

    dq = lax.fori_loop(0, count, backward, jnp.zeros((stacked, DH), jnp.float32)) * scale
    for g in range(heads):
        dq_ref[:, g * DH : (g + 1) * DH] = dq[g * rows : (g + 1) * rows]

    @pl.when(span == pl.num_programs(1) - 1)
    def _():
        dk_ref[...] = dk_ref[...] * scale


def attention(span_list, span_count, query, grad, keys, values, qpos, qdoc, kpos, kdoc, interpret=False):
    rows, width = query.shape
    keys_len, kv_width = keys.shape
    groups = width // kv_width
    heads = kv_width // DH
    q_spec = pl.BlockSpec((QUERY_ROWS, groups * DH), lambda c, s, *_: (s, c))
    k_spec = pl.BlockSpec((keys_len, DH), lambda c, s, *_: (0, c))
    col_spec = pl.BlockSpec((QUERY_ROWS, 1), lambda c, s, *_: (s, 0))
    row_spec = pl.BlockSpec((1, keys_len), lambda c, s, *_: (0, 0))
    return pl.pallas_call(
        attention_kernel,
        grid_spec=pltpu.PrefetchScalarGridSpec(
            num_scalar_prefetch=2,
            grid=(heads, rows // QUERY_ROWS),
            in_specs=[q_spec, q_spec, k_spec, k_spec, col_spec, col_spec, row_spec, row_spec],
            out_specs=[q_spec, k_spec, k_spec],
            scratch_shapes=[pltpu.VMEM((keys_len // SPAN_ROWS, groups * QUERY_ROWS, SPAN_ROWS), jnp.float32)],
        ),
        out_shape=[
            jax.ShapeDtypeStruct((rows, width), jnp.float32),
            jax.ShapeDtypeStruct((keys_len, kv_width), jnp.float32),
            jax.ShapeDtypeStruct((keys_len, kv_width), jnp.float32),
        ],
        compiler_params=pltpu.CompilerParams(
            dimension_semantics=("arbitrary", "arbitrary"), vmem_limit_bytes=48 * 1024 * 1024
        ),
        interpret=interpret,
    )(span_list, span_count, query, grad, keys, values, qpos, qdoc, kpos, kdoc)


def visible(query_pos, query_doc, key_pos, key_doc):
    return (key_pos[None, :] <= query_pos[:, None]) & (key_doc[None, :] == query_doc[:, None])


def local(query_in, key_in, value_in, grad_out, target, span_order, doc_ids):
    local_rows = query_in.shape[0]
    devices = lax.axis_size(("dp", "ctx"))
    ctx_size = lax.axis_size("ctx")
    packs = devices // ctx_size
    pack_len = local_rows * ctx_size
    capacity = (local_rows // devices + 2) * ctx_size
    q_cols = query_in.shape[1]
    k_cols = key_in.shape[1]
    q_width = q_cols // ctx_size
    k_width = k_cols // ctx_size
    ctx_ids = np.arange(ctx_size)
    kv_of = (ctx_ids // 4) * 2 + ctx_ids % 2
    half_of = (ctx_ids // 2) % 2
    block_of = 2 * kv_of + half_of
    ctx_of_block = np.argsort(block_of)

    pack_of = target // pack_len
    row_in_pack = target % pack_len
    onehot = (pack_of[:, None] == jnp.arange(packs, dtype=jnp.int32)[None, :]).astype(jnp.int32)
    slot = jnp.sum((jnp.cumsum(onehot, axis=0) - onehot) * onehot, axis=1)
    dest_pack = pack_of[:, None]
    dest_ctx = jnp.asarray(ctx_ids, jnp.int32)[None, :]
    dest_slot = slot[:, None]

    payload = jnp.concatenate(
        [
            query_in.reshape(local_rows, ctx_size, q_width)[:, block_of],
            grad_out.reshape(local_rows, ctx_size, q_width)[:, block_of],
            key_in.reshape(local_rows, k_cols // DH, DH)[:, kv_of],
            value_in.reshape(local_rows, k_cols // DH, DH)[:, kv_of],
        ],
        axis=2,
    )
    width = payload.shape[2]
    flat_slot = pack_of * capacity + slot
    picks = jnp.arange(packs * capacity, dtype=jnp.int32)[:, None] == flat_slot[None, :]
    holder = (
        jnp.dot(
            picks.astype(jnp.bfloat16),
            payload.reshape(local_rows, ctx_size * width),
            preferred_element_type=jnp.float32,
        )
        .astype(jnp.bfloat16)
        .reshape(packs, capacity, ctx_size, width)
        .transpose(0, 2, 1, 3)
        .reshape(devices * capacity, width)
    )
    places = jnp.broadcast_to(
        jnp.sum(jnp.where(picks, (row_in_pack + 1)[None, :], 0), axis=1).reshape(packs, 1, capacity),
        (packs, ctx_size, capacity),
    ).reshape(devices * capacity)
    got = lax.all_to_all(holder, ("dp", "ctx"), split_axis=0, concat_axis=0, tiled=True)
    got_places = lax.all_to_all(places, ("dp", "ctx"), split_axis=0, concat_axis=0, tiled=True)
    span_seq = span_order[0]
    span_rows = pack_len // span_seq.shape[0]
    packed_row = got_places - 1
    span_pos = jnp.sum(
        jnp.where(
            (packed_row // span_rows)[:, None] == jnp.arange(span_seq.shape[0], dtype=jnp.int32)[None, :],
            span_seq[None, :],
            0,
        ),
        axis=1,
    )
    landing = jnp.where(packed_row >= 0, span_pos * span_rows + packed_row % span_rows, pack_len)
    lands = jnp.arange(pack_len, dtype=jnp.int32)[:, None] == landing[None, :]
    rows = jnp.dot(lands.astype(jnp.bfloat16), got, preferred_element_type=jnp.float32).astype(jnp.bfloat16)
    query = rows[:, :q_width]
    grad_rows = rows[:, q_width : 2 * q_width]
    keys = rows[:, 2 * q_width : 2 * q_width + DH]
    values = rows[:, 2 * q_width + DH : 2 * q_width + 2 * DH]

    doc_block = jnp.broadcast_to(doc_ids[0].astype(jnp.bfloat16)[:, None], (local_rows, 128))
    doc_all = lax.all_gather(doc_block, "ctx", axis=0, tiled=True)[:, 0].astype(jnp.int32)
    positions = jnp.arange(pack_len, dtype=jnp.int32)

    spans = pack_len // SPAN_ROWS
    query_tiles = pack_len // QUERY_ROWS
    tile_docs = doc_all.reshape(spans, SPAN_ROWS)
    query_docs = doc_all.reshape(query_tiles, QUERY_ROWS)
    tile_ids = jnp.arange(spans)
    query_ids = jnp.arange(query_tiles)
    active = (
        (tile_ids[None, :] * SPAN_ROWS < (query_ids[:, None] + 1) * QUERY_ROWS)
        & (tile_docs[None, :, 0] <= query_docs[:, None, -1])
        & (query_docs[:, None, 0] <= tile_docs[None, :, -1])
    )
    span_count = jnp.sum(active.astype(jnp.int32), axis=1)
    rank = jnp.cumsum(active.astype(jnp.int32), axis=1) - 1
    slot_of = jnp.where(active, rank + spans * query_ids[:, None], spans * query_tiles)
    span_list = (
        jnp.zeros((spans * query_tiles,), jnp.int32)
        .at[slot_of.reshape(-1)]
        .set(jnp.tile(jnp.arange(spans, dtype=jnp.int32), query_tiles), mode="drop")
    )
    dquery, dkey, dvalue = attention(
        span_list,
        span_count,
        query,
        grad_rows,
        keys,
        values,
        positions.reshape(pack_len, 1),
        doc_all.reshape(pack_len, 1),
        positions.reshape(1, pack_len),
        doc_all.reshape(1, pack_len),
    )

    half = jnp.asarray(half_of, jnp.int32)[lax.axis_index("ctx")]
    split_key = dkey.reshape(pack_len, 2, k_width)
    split_value = dvalue.reshape(pack_len, 2, k_width)
    mine = jnp.concatenate(
        [lax.dynamic_index_in_dim(split_key, half, 1, False), lax.dynamic_index_in_dim(split_value, half, 1, False)],
        axis=1,
    )
    other = jnp.concatenate(
        [
            lax.dynamic_index_in_dim(split_key, 1 - half, 1, False),
            lax.dynamic_index_in_dim(split_value, 1 - half, 1, False),
        ],
        axis=1,
    ).astype(jnp.bfloat16)
    partner = [(int(c), int(c) ^ 2) for c in ctx_ids]
    key_value = mine + lax.ppermute(other, "ctx", partner).astype(jnp.float32)

    result = jnp.concatenate([dquery.astype(jnp.bfloat16), key_value.astype(jnp.bfloat16)], axis=1)
    back = lax.all_to_all(
        lax.dot_general(
            lands.astype(jnp.bfloat16), result, (((0,), (0,)), ((), ())), preferred_element_type=jnp.float32
        ).astype(jnp.bfloat16),
        ("dp", "ctx"),
        split_axis=0,
        concat_axis=0,
        tiled=True,
    ).reshape(packs, ctx_size, capacity, result.shape[1])[:, ctx_of_block]
    pieces = lax.dot_general(
        picks.T.reshape(local_rows, packs, capacity).astype(jnp.bfloat16),
        back,
        (((1, 2), (0, 2)), ((), ())),
        preferred_element_type=jnp.float32,
    )
    return (
        pieces[:, :, :q_width].reshape(local_rows, q_cols),
        pieces[:, :, q_width : q_width + k_width].reshape(local_rows, k_cols),
        pieces[:, :, q_width + k_width :].reshape(local_rows, k_cols),
    )


def solution(mesh):
    placed = (
        P(("dp", "ctx"), None),
        P(("dp", "ctx"), None),
        P(("dp", "ctx"), None),
        P(("dp", "ctx"), None),
        P(("dp", "ctx")),
        P("dp", None),
        P("dp", "ctx"),
    )
    return jax.shard_map(
        local,
        mesh=mesh,
        in_specs=placed,
        out_specs=(P(("dp", "ctx"), None), P(("dp", "ctx"), None), P(("dp", "ctx"), None)),
        check_vma=False,
    )
```

```python
import jax
import numpy as np
import jax.numpy as jnp
from jax import lax
from jax.sharding import PartitionSpec as P
from jax.experimental import pallas as pl
from jax.experimental.pallas import tpu as pltpu

HQ = 16
HK = 4
DH = 128


SPAN_ROWS = 256
QUERY_ROWS = 512


def attention_kernel(
    list_ref, count_ref, q_ref, g_ref, k_ref, v_ref, qpos_ref, qdoc_ref, kpos_ref, kdoc_ref,
    dq_ref, dk_ref, dv_ref, tiles_ref,
):
    scale = DH ** (-0.5)
    rows = q_ref.shape[0]
    heads = q_ref.shape[1] // DH
    stacked = heads * rows
    span = pl.program_id(1)
    spans = list_ref.shape[0] // pl.num_programs(1)
    count = count_ref[span]

    @pl.when(span == 0)
    def _():
        dk_ref[...] = jnp.zeros(dk_ref.shape, jnp.float32)
        dv_ref[...] = jnp.zeros(dv_ref.shape, jnp.float32)

    qpos = qpos_ref[...]
    qdoc = qdoc_ref[...]
    q = jnp.concatenate([q_ref[:, g * DH : (g + 1) * DH] for g in range(heads)], axis=0)
    gr = jnp.concatenate([g_ref[:, g * DH : (g + 1) * DH] for g in range(heads)], axis=0)

    def first_key(i):
        return pl.multiple_of(list_ref[span * spans + i] * SPAN_ROWS, SPAN_ROWS)

    def stats(i, carry):
        m, l = carry
        start = first_key(i)
        kp = kpos_ref[:, pl.ds(start, SPAN_ROWS)]
        kd = kdoc_ref[:, pl.ds(start, SPAN_ROWS)]
        allowed = (kp <= qpos) & (kd == qdoc)
        s = lax.dot_general(
            q, k_ref[pl.ds(start, SPAN_ROWS), :], (((1,), (1,)), ((), ())),
            preferred_element_type=jnp.float32,
        ) * scale
        s = jnp.where(allowed[None], s.reshape(heads, rows, SPAN_ROWS), -jnp.inf).reshape(stacked, SPAN_ROWS)
        tiles_ref[i] = s
        m_new = jnp.maximum(m, jnp.max(s, axis=1, keepdims=True))
        l = l * jnp.exp(m - m_new) + jnp.sum(jnp.exp(s - m_new), axis=1, keepdims=True)
        return m_new, l

    m, l = lax.fori_loop(
        0, count, stats, (jnp.full((stacked, 1), -1e30, jnp.float32), jnp.zeros((stacked, 1), jnp.float32))
    )
    lse = m + jnp.log(l)

    def forward(i, o):
        start = first_key(i)
        p = jnp.exp(tiles_ref[i] - lse)
        tiles_ref[i] = p
        return o + jnp.dot(
            p.astype(jnp.bfloat16), v_ref[pl.ds(start, SPAN_ROWS), :], preferred_element_type=jnp.float32
        )

    o = lax.fori_loop(0, count, forward, jnp.zeros((stacked, DH), jnp.float32))
    delta = jnp.sum(gr.astype(jnp.float32) * o.astype(jnp.bfloat16).astype(jnp.float32), axis=1, keepdims=True)

    def backward(i, dq):
        start = first_key(i)
        kb = k_ref[pl.ds(start, SPAN_ROWS), :]
        vb = v_ref[pl.ds(start, SPAN_ROWS), :]
        p = tiles_ref[i]
        dp = lax.dot_general(gr, vb, (((1,), (1,)), ((), ())), preferred_element_type=jnp.float32)
        ds = (p * (dp - delta)).astype(jnp.bfloat16)
        dk_ref[pl.ds(start, SPAN_ROWS), :] += lax.dot_general(
            ds, q, (((0,), (0,)), ((), ())), preferred_element_type=jnp.float32
        )
        dv_ref[pl.ds(start, SPAN_ROWS), :] += lax.dot_general(
            p.astype(jnp.bfloat16), gr, (((0,), (0,)), ((), ())), preferred_element_type=jnp.float32
        )
        return dq + jnp.dot(ds, kb, preferred_element_type=jnp.float32)

    dq = lax.fori_loop(0, count, backward, jnp.zeros((stacked, DH), jnp.float32)) * scale
    for g in range(heads):
        dq_ref[:, g * DH : (g + 1) * DH] = dq[g * rows : (g + 1) * rows]

    @pl.when(span == pl.num_programs(1) - 1)
    def _():
        dk_ref[...] = dk_ref[...] * scale


def attention(span_list, span_count, query, grad, keys, values, qpos, qdoc, kpos, kdoc, interpret=False):
    rows, width = query.shape
    keys_len, kv_width = keys.shape
    groups = width // kv_width
    heads = kv_width // DH
    q_spec = pl.BlockSpec((QUERY_ROWS, groups * DH), lambda c, s, *_: (s, c))
    k_spec = pl.BlockSpec((keys_len, DH), lambda c, s, *_: (0, c))
    col_spec = pl.BlockSpec((QUERY_ROWS, 1), lambda c, s, *_: (s, 0))
    row_spec = pl.BlockSpec((1, keys_len), lambda c, s, *_: (0, 0))
    return pl.pallas_call(
        attention_kernel,
        grid_spec=pltpu.PrefetchScalarGridSpec(
            num_scalar_prefetch=2,
            grid=(heads, rows // QUERY_ROWS),
            in_specs=[q_spec, q_spec, k_spec, k_spec, col_spec, col_spec, row_spec, row_spec],
            out_specs=[q_spec, k_spec, k_spec],
            scratch_shapes=[pltpu.VMEM((keys_len // SPAN_ROWS, groups * QUERY_ROWS, SPAN_ROWS), jnp.float32)],
        ),
        out_shape=[
            jax.ShapeDtypeStruct((rows, width), jnp.float32),
            jax.ShapeDtypeStruct((keys_len, kv_width), jnp.float32),
            jax.ShapeDtypeStruct((keys_len, kv_width), jnp.float32),
        ],
        compiler_params=pltpu.CompilerParams(
            dimension_semantics=("arbitrary", "arbitrary"), vmem_limit_bytes=48 * 1024 * 1024
        ),
        interpret=interpret,
    )(span_list, span_count, query, grad, keys, values, qpos, qdoc, kpos, kdoc)


def visible(query_pos, query_doc, key_pos, key_doc):
    return (key_pos[None, :] <= query_pos[:, None]) & (key_doc[None, :] == query_doc[:, None])


def local(query_in, key_in, value_in, grad_out, target, span_order, doc_ids):
    local_rows = query_in.shape[0]
    devices = lax.axis_size(("dp", "ctx"))
    ctx_size = lax.axis_size("ctx")
    packs = devices // ctx_size
    pack_len = local_rows * ctx_size
    capacity = (local_rows // devices + 2) * ctx_size
    q_cols = query_in.shape[1]
    k_cols = key_in.shape[1]
    q_width = q_cols // ctx_size
    k_width = k_cols // ctx_size
    ctx_ids = np.arange(ctx_size)
    kv_of = ctx_ids // 2
    half_of = ctx_ids % 2

    pack_of = target // pack_len
    row_in_pack = target % pack_len
    onehot = (pack_of[:, None] == jnp.arange(packs, dtype=jnp.int32)[None, :]).astype(jnp.int32)
    slot = jnp.sum((jnp.cumsum(onehot, axis=0) - onehot) * onehot, axis=1)
    dest_pack = pack_of[:, None]
    dest_ctx = jnp.asarray(ctx_ids, jnp.int32)[None, :]
    dest_slot = slot[:, None]

    payload = jnp.concatenate(
        [
            query_in.reshape(local_rows, ctx_size, q_width),
            grad_out.reshape(local_rows, ctx_size, q_width),
            key_in.reshape(local_rows, k_cols // DH, DH)[:, kv_of],
            value_in.reshape(local_rows, k_cols // DH, DH)[:, kv_of],
        ],
        axis=2,
    )
    width = payload.shape[2]
    flat_slot = pack_of * capacity + slot
    picks = jnp.arange(packs * capacity, dtype=jnp.int32)[:, None] == flat_slot[None, :]
    holder = (
        jnp.dot(
            picks.astype(jnp.bfloat16),
            payload.reshape(local_rows, ctx_size * width),
            preferred_element_type=jnp.float32,
        )
        .astype(jnp.bfloat16)
        .reshape(packs, capacity, ctx_size, width)
        .transpose(0, 2, 1, 3)
        .reshape(devices * capacity, width)
    )
    places = jnp.broadcast_to(
        jnp.sum(jnp.where(picks, (row_in_pack + 1)[None, :], 0), axis=1).reshape(packs, 1, capacity),
        (packs, ctx_size, capacity),
    ).reshape(devices * capacity)
    got = lax.all_to_all(holder, ("dp", "ctx"), split_axis=0, concat_axis=0, tiled=True)
    got_places = lax.all_to_all(places, ("dp", "ctx"), split_axis=0, concat_axis=0, tiled=True)
    span_seq = span_order[0]
    span_rows = pack_len // span_seq.shape[0]
    packed_row = got_places - 1
    span_pos = jnp.sum(
        jnp.where(
            (packed_row // span_rows)[:, None] == jnp.arange(span_seq.shape[0], dtype=jnp.int32)[None, :],
            span_seq[None, :],
            0,
        ),
        axis=1,
    )
    landing = jnp.where(packed_row >= 0, span_pos * span_rows + packed_row % span_rows, pack_len)
    lands = jnp.arange(pack_len, dtype=jnp.int32)[:, None] == landing[None, :]
    rows = jnp.dot(lands.astype(jnp.bfloat16), got, preferred_element_type=jnp.float32).astype(jnp.bfloat16)
    query = rows[:, :q_width]
    grad_rows = rows[:, q_width : 2 * q_width]
    keys = rows[:, 2 * q_width : 2 * q_width + DH]
    values = rows[:, 2 * q_width + DH : 2 * q_width + 2 * DH]

    doc_block = jnp.broadcast_to(doc_ids[0].astype(jnp.bfloat16)[:, None], (local_rows, 128))
    doc_all = lax.all_gather(doc_block, "ctx", axis=0, tiled=True)[:, 0].astype(jnp.int32)
    positions = jnp.arange(pack_len, dtype=jnp.int32)

    spans = pack_len // SPAN_ROWS
    query_tiles = pack_len // QUERY_ROWS
    tile_docs = doc_all.reshape(spans, SPAN_ROWS)
    query_docs = doc_all.reshape(query_tiles, QUERY_ROWS)
    tile_ids = jnp.arange(spans)
    query_ids = jnp.arange(query_tiles)
    active = (
        (tile_ids[None, :] * SPAN_ROWS < (query_ids[:, None] + 1) * QUERY_ROWS)
        & (tile_docs[None, :, 0] <= query_docs[:, None, -1])
        & (query_docs[:, None, 0] <= tile_docs[None, :, -1])
    )
    span_count = jnp.sum(active.astype(jnp.int32), axis=1)
    rank = jnp.cumsum(active.astype(jnp.int32), axis=1) - 1
    slot_of = jnp.where(active, rank + spans * query_ids[:, None], spans * query_tiles)
    span_list = (
        jnp.zeros((spans * query_tiles,), jnp.int32)
        .at[slot_of.reshape(-1)]
        .set(jnp.tile(jnp.arange(spans, dtype=jnp.int32), query_tiles), mode="drop")
    )
    dquery, dkey, dvalue = attention(
        span_list,
        span_count,
        query,
        grad_rows,
        keys,
        values,
        positions.reshape(pack_len, 1),
        doc_all.reshape(pack_len, 1),
        positions.reshape(1, pack_len),
        doc_all.reshape(1, pack_len),
    )

    half = jnp.asarray(half_of, jnp.int32)[lax.axis_index("ctx")]
    split_key = dkey.reshape(pack_len, 2, k_width)
    split_value = dvalue.reshape(pack_len, 2, k_width)
    mine = jnp.concatenate(
        [lax.dynamic_index_in_dim(split_key, half, 1, False), lax.dynamic_index_in_dim(split_value, half, 1, False)],
        axis=1,
    )
    other = jnp.concatenate(
        [
            lax.dynamic_index_in_dim(split_key, 1 - half, 1, False),
            lax.dynamic_index_in_dim(split_value, 1 - half, 1, False),
        ],
        axis=1,
    ).astype(jnp.bfloat16)
    partner = [(int(c), int(c) ^ 1) for c in ctx_ids]
    key_value = mine + lax.ppermute(other, "ctx", partner).astype(jnp.float32)

    result = jnp.concatenate([dquery.astype(jnp.bfloat16), key_value.astype(jnp.bfloat16)], axis=1)
    back = lax.all_to_all(
        lax.dot_general(
            lands.astype(jnp.bfloat16), result, (((0,), (0,)), ((), ())), preferred_element_type=jnp.float32
        ).astype(jnp.bfloat16),
        ("dp", "ctx"),
        split_axis=0,
        concat_axis=0,
        tiled=True,
    ).reshape(packs, ctx_size, capacity, result.shape[1])
    pieces = lax.dot_general(
        picks.T.reshape(local_rows, packs, capacity).astype(jnp.bfloat16),
        back,
        (((1, 2), (0, 2)), ((), ())),
        preferred_element_type=jnp.float32,
    )
    return (
        pieces[:, :, :q_width].reshape(local_rows, q_cols),
        pieces[:, :, q_width : q_width + k_width].reshape(local_rows, k_cols),
        pieces[:, :, q_width + k_width :].reshape(local_rows, k_cols),
    )


def solution(mesh):
    placed = (
        P(("dp", "ctx"), None),
        P(("dp", "ctx"), None),
        P(("dp", "ctx"), None),
        P(("dp", "ctx"), None),
        P(("dp", "ctx")),
        P("dp", None),
        P("dp", "ctx"),
    )
    return jax.shard_map(
        local,
        mesh=mesh,
        in_specs=placed,
        out_specs=(P(("dp", "ctx"), None), P(("dp", "ctx"), None), P(("dp", "ctx"), None)),
        check_vma=False,
    )
```
